1024 devices in a mesh: tile: 64 (over z, y_hi, core), thick: 4 (over x), rve: 4 (over y_lo).
Axes of the slice: x: 4, y: 8 (y_hi: 2, y_lo: 4; y = y_hi * 4 + y_lo), z: 16, core: 2. Of those that a mesh axis runs over, the one named last changes fastest.
Arguments:
- gen_strain: float32 [6, 2048], P(None, 'tile'), may hold values from -2.5 to 2.5
- ply_class: int32 [8], replicated, may hold values from 0 to 3
- route: int32 [4, 2048, 2, 1], P('thick', 'tile'), may hold values from 0 to 63; in each aligned block of 64 rows (0 to 63, 64 to 127, ..., all dimensions but the last counted through in order) at most 2 rows name the same one
- phase: int32 [4, 16, 16, 16], P(None, 'rve'), may hold values from 0 to 1
- rve_state: float32 [3, 16, 16, 16, 32768], P(None, 'rve', None, None, ('tile', 'thick')), may hold values from -2.5 to 2.5
- connect: int32 [4, 2048], P(None, 'tile'), may hold values from 0 to 39
- bmat: float32 [4, 6, 6, 2048], P(None, None, None, 'tile'), may hold values from -2.5 to 2.5
- velocity: float32 [6, 2048], P(None, 'tile'), may hold values from -6 to 6
- force_ext: float32 [6, 2048], P(None, 'tile'), may hold values from -6 to 6
- mass: float32 [2048], P('tile'), may hold values from 0.5 to 2
Outputs:
- new_velocity: float32 [6, 2048], P(None, 'tile')
- resultants: float32 [6, 2048], P(None, 'tile')
- new_state: float32 [3, 16, 16, 16, 32768], P(None, 'rve', None, None, ('tile', 'thick'))
The draws below stay inside these ranges and needn't reach their ends.
Inputs may be any that keep to these rules, and one draw needn't show every extreme that they name: `route`: among the rows of one device (32 elements times 2 points) no tile is named more than 2 times, a bound that some block reaches. `connect`: A value below 32 is a node of the element's own tile; 32 + j is node j of the next tile.
All inputs are finite; a program needn't handle non-finite values.
Results may differ from the reference program's by a relative error of at most 0.000098.
Values sent between devices are 32-bit elements; how exact they have to be, the bound alone decides.
No kernel may reach another device: no remote copies, remote signals or barrier semaphores. Data moves between devices by JAX's collectives and lax.ppermute only.
A program may use at most 32 MiB of HBM per device.

```python
import math
import jax
import jax.numpy as jnp
import numpy as np
from jax import lax

E_DEV = 32
TP = 8
TPG = 2
NCLASS = 4
RES = 16
ITERS = 2
GHOST = 8
NODE_DEV = 32
CAP = 2
SLOTS = 128
ELEMS = 2048
NODES = 2048
N_TILE = 64
N_THICK = 4


def touch_ends(values, rng, least, high):
    spot = [jax.random.randint(jax.random.fold_in(rng, axis), (), 0, length) for axis, length in enumerate(values.shape)]
    main_axis = values.shape.index(max(values.shape))
    neighbour = spot[:main_axis] + [(spot[main_axis] + 1) % values.shape[main_axis]] + spot[main_axis + 1:]
    return values.at[tuple(spot)].set(least).at[tuple(neighbour)].set(high)


def block_levels(key, extent, cuts, least, high):
    def one(position, parts):
        steps = jax.random.uniform(jax.random.fold_in(jax.random.fold_in(key, 6), position), (parts,), jnp.float32, least / len(cuts), high / len(cuts))
        return jnp.repeat(jnp.exp(steps), extent[position] // parts).reshape((-1,) + (1,) * (len(extent) - position - 1))

    loudness = one(*cuts[0])
    for cut in cuts[1:]:
        loudness = loudness * one(*cut)
    return loudness


def shared_out(rng, own, number, rows, number_of, top, bound, slope):
    ranking = jax.random.permutation(rng, number_of)
    heavy_load, common = load_shares(number_of, rows * top, bound, slope, True), load_shares(number_of, rows * top, bound, slope, False)
    places = jnp.arange(number_of)

    def named(lengths, rotation):
        used = int((lengths > 0).sum())
        fixed = max(1, used // 4)
        shifted = fixed + (places - fixed + rotation * (used - fixed)) % max(1, number_of - fixed)
        return jnp.zeros((number_of,), jnp.int32).at[ranking[jnp.where(places < fixed, places, shifted)]].set(jnp.asarray(lengths, jnp.int32))

    lengths = jnp.where(number % 4 == 0, named(heavy_load, number // 4), named(common, number - number // 4 - 1))
    mixed = jax.random.permutation(jax.random.fold_in(own, 3), number_of)
    source_of, taker = mixed[0:number_of // 2 * 2:2], mixed[1:number_of // 2 * 2:2]
    room = jnp.minimum(lengths[source_of] - 1, bound - lengths[taker]) // 2
    room = jnp.where((source_of == ranking[0]) | (taker == ranking[0]) | (lengths[taker] == 0), 0, jnp.maximum(room, 0))
    shifted = jax.random.randint(jax.random.fold_in(own, 4), (number_of // 2,), 0, 1 << 20) % (room + 1)
    lengths = lengths.at[source_of].add(-shifted).at[taker].add(shifted)
    labels = jnp.searchsorted(jnp.cumsum(lengths), jnp.arange(rows * top), side="right").astype(jnp.int32)
    grid = labels.reshape(top, rows).T
    grid = grid[jax.random.permutation(jax.random.fold_in(own, 1), rows)]
    rotation = jax.random.randint(jax.random.fold_in(own, 2), (rows, 1), 0, top)
    return jnp.take_along_axis(grid, (jnp.arange(top)[None, :] + rotation) % top, axis=1)


def load_shares(count, total, reach, lean, full):
    weights = [(1 << 20) // math.isqrt(grade ** lean) + 1 for grade in range(1, count + 1)]
    largest = reach if full else min(reach, max(-(-total // count), total * weights[0] // sum(weights)))
    least = 1 if total - largest >= count - 1 else 0
    counts, surplus = [largest] + [least] * (count - 1), total - largest - least * (count - 1)
    while surplus > 0:
        movable = [i for i in range(1, count) if counts[i] < largest] or [i for i in range(1, count) if counts[i] < reach]
        whole, left = sum([weights[i] for i in movable]), surplus
        for i in movable:
            more = min(reach - counts[i], max(1, left * weights[i] // whole), surplus)
            counts[i] = counts[i] + more
            surplus = surplus - more
    return np.array(counts)


def noise(stream_key, extent, scale, limit, shards=(), kind=jnp.bfloat16):
    gain = block_levels(stream_key, extent, shards, -0.22, 0.18) if shards else 1.0
    values = jax.random.normal(stream_key, extent, jnp.float32) * scale * gain
    return jnp.minimum(jnp.maximum(values, -limit), limit).astype(kind)


def setup_inputs(seed: int = 0) -> dict:
    keys = jax.random.split(jax.random.key(seed), 11)
    gen_strain = noise(keys[0], (6, ELEMS), 0.2, 2.5, ((1, 64),), jnp.float32)
    ply_class = touch_ends(jax.random.randint(keys[1], (TP,), 0, NCLASS), jax.random.fold_in(keys[1], 1), 0, NCLASS - 1).astype(jnp.int32)
    route_keys = jax.random.split(jax.random.fold_in(keys[2], 1), N_THICK * ELEMS * TPG // (E_DEV * TPG))
    route_turns = jax.random.permutation(jax.random.fold_in(keys[2], 3), N_THICK * ELEMS * TPG // (E_DEV * TPG))
    route = jax.vmap(lambda own, number: shared_out(jax.random.fold_in(keys[2], 2), own, number, E_DEV * TPG, N_TILE, 1, CAP, 2))(route_keys, route_turns).reshape((N_THICK, ELEMS, TPG, 1))
    phase = touch_ends(jax.random.randint(keys[3], (NCLASS, RES, RES, RES), 0, 2), jax.random.fold_in(keys[3], 1), 0, 1).astype(jnp.int32)
    rve_state = noise(keys[4], (3, RES, RES, RES, N_TILE * N_THICK * SLOTS), 0.3, 2.5, ((1, 4), (4, 256)), jnp.float32)
    connect = touch_ends(jax.random.randint(keys[5], (4, ELEMS), 0, NODE_DEV + GHOST), jax.random.fold_in(keys[5], 1), 0, (NODE_DEV + GHOST) - 1).astype(jnp.int32)
    bmat = noise(keys[6], (4, 6, 6, ELEMS), 6 ** -0.5, 2.5, ((3, 64),), jnp.float32)
    velocity = noise(keys[7], (6, NODES), 1.0, 6.0, ((1, 64),), jnp.float32)
    force_ext = noise(keys[8], (6, NODES), 1.0, 6.0, ((1, 64),), jnp.float32)
    mass = jnp.clip(jnp.exp(math.log(2.0) - 1.3862944 * jax.random.uniform(keys[9], (NODES,), jnp.float32) ** block_levels(keys[9], (NODES,), ((0, 64),), -0.2, 0.2)), 0.5, 2.0)
    return dict(gen_strain=gen_strain, ply_class=ply_class, route=route, phase=phase, rve_state=rve_state, connect=connect, bmat=bmat, velocity=velocity, force_ext=force_ext, mass=mass)


matrix_lame = 1.2
matrix_shear = 0.8
fiber_lame = 8.0
fiber_shear = 5.0
relax_rate = 1.0 / 288.0
time_step = 0.25


def material_stress(grads, lame_field, shear_field, macro):
    eps11 = macro[0] + grads[0][0]
    eps22 = macro[1] + grads[1][1]
    eps33 = grads[2][2]
    eps12 = macro[2] + 0.5 * (grads[0][1] + grads[1][0])
    eps13 = 0.5 * (grads[0][2] + grads[2][0])
    eps23 = 0.5 * (grads[1][2] + grads[2][1])
    volume = lame_field * (eps11 + eps22 + eps33)
    twice = 2.0 * shear_field
    return (volume + twice * eps11, volume + twice * eps22, volume + twice * eps33,
            twice * eps12, twice * eps13, twice * eps23)


def rotate_in(strain, cosine, sine):
    first, second, shear = strain[0], strain[1], strain[2]
    return jnp.stack([
        cosine * cosine * first + sine * sine * second + 2.0 * cosine * sine * shear,
        sine * sine * first + cosine * cosine * second - 2.0 * cosine * sine * shear,
        -cosine * sine * first + cosine * sine * second + (cosine * cosine - sine * sine) * shear])


def rotate_out(stress, cosine, sine):
    first, second, shear = stress[0], stress[1], stress[2]
    return jnp.stack([
        cosine * cosine * first + sine * sine * second - 2.0 * cosine * sine * shear,
        sine * sine * first + cosine * cosine * second + 2.0 * cosine * sine * shear,
        cosine * sine * first - cosine * sine * second + (cosine * cosine - sine * sine) * shear])


def backward(field, axis):
    return field - jnp.roll(field, 1, axis)


def relax_full(state, lame_field, shear_field, macro):
    grads = [[jnp.roll(state[i], -1, j) - state[i] for j in range(3)] for i in range(3)]
    s11, s22, s33, s12, s13, s23 = material_stress(grads, lame_field, shear_field, macro)
    first = backward(s11, 0) + backward(s12, 1) + backward(s13, 2)
    second = backward(s12, 0) + backward(s22, 1) + backward(s23, 2)
    third = backward(s13, 0) + backward(s23, 1) + backward(s33, 2)
    new_state = state + relax_rate * jnp.stack([first, second, third])
    return new_state, (s11, s22, s12)


def reference(gen_strain, ply_class, route, phase, rve_state, connect, bmat, velocity, force_ext, mass):
    highest = lax.Precision.HIGHEST
    layer = jnp.arange(TP, dtype=jnp.int32).reshape(N_THICK, TPG)
    heights = -1.0 + (2.0 * layer.astype(jnp.float32) + 1.0) / TP
    classes = ply_class.reshape(N_THICK, TPG)
    angle = classes.astype(jnp.float32) * (math.pi / NCLASS)
    cosine = jnp.cos(angle)[:, None, :]
    sine = jnp.sin(angle)[:, None, :]
    membrane = gen_strain[:3][:, None, :, None]
    bending = gen_strain[3:][:, None, :, None]
    point_strain = membrane + heights[None, :, None, :] * bending
    rotated = rotate_in(point_strain, cosine, sine)
    target = route[..., 0].reshape(N_THICK, N_TILE, E_DEV * TPG)
    tile_hot = (target[..., None] == jnp.arange(N_TILE, dtype=jnp.int32)).astype(jnp.int32)
    rank = jnp.sum((jnp.cumsum(tile_hot, axis=2) - 1) * tile_hot, axis=3)
    thick_ids = jnp.arange(N_THICK, dtype=jnp.int32)[:, None, None]
    source = jnp.arange(N_TILE, dtype=jnp.int32)[None, :, None]
    slot = ((target * N_THICK + thick_ids) * SLOTS + source * CAP + rank).reshape(-1)
    total = N_TILE * N_THICK * SLOTS
    slot_macro = jnp.zeros((total, 3), jnp.float32).at[slot].set(rotated.reshape(3, -1).T)
    point_class = jnp.broadcast_to(classes[:, None, :], (N_THICK, ELEMS, TPG)).reshape(-1)
    slot_class = jnp.zeros((total,), jnp.int32).at[slot].set(point_class)
    lame_class = jnp.where(phase == 1, fiber_lame, matrix_lame).astype(jnp.float32)
    shear_class = jnp.where(phase == 1, fiber_shear, matrix_shear).astype(jnp.float32)
    blocks = N_TILE * N_THICK
    states = jnp.moveaxis(rve_state.reshape(3, RES, RES, RES, blocks, SLOTS), 4, 0)
    macros = slot_macro.reshape(blocks, SLOTS, 3)
    block_classes = slot_class.reshape(blocks, SLOTS)

    def solve_block(pieces):
        state, macro_rows, class_rows = pieces
        lame_field = jnp.moveaxis(lame_class[class_rows], 0, -1)
        shear_field = jnp.moveaxis(shear_class[class_rows], 0, -1)
        macro = macro_rows.T
        stress = None
        for sweep_number in range(ITERS):
            state, stress = relax_full(state, lame_field, shear_field, macro)
        average = jnp.stack([jnp.sum(part, axis=(0, 1, 2)) for part in stress]) / float(RES ** 3)
        return state, average.T

    new_states, averages = lax.map(solve_block, (states, macros, block_classes))
    new_state = jnp.moveaxis(new_states, 0, 4).reshape(3, RES, RES, RES, total)
    point_stress = averages.reshape(total, 3)[slot]
    point_stress = point_stress.T.reshape(3, N_THICK, ELEMS, TPG)
    global_stress = rotate_out(point_stress, cosine, sine)
    weight = 1.0 / TP
    forces = jnp.sum(global_stress, axis=(1, 3)) * weight
    moments = jnp.sum(global_stress * heights[None, :, None, :], axis=(1, 3)) * weight
    resultants = jnp.concatenate([forces, moments], 0)
    corner_force = jnp.einsum("akme,me->ake", bmat, resultants, precision=highest)
    tile_of = (jnp.arange(ELEMS, dtype=jnp.int32) // E_DEV)[None, :]
    node_ids = jnp.where(connect < NODE_DEV, tile_of * NODE_DEV + connect,
                         ((tile_of + 1) % N_TILE) * NODE_DEV + connect - NODE_DEV)
    data = jnp.transpose(corner_force, (0, 2, 1)).reshape(-1, 6)
    internal = jax.ops.segment_sum(data, node_ids.reshape(-1), num_segments=NODES).T
    new_velocity = velocity + time_step * (force_ext - internal) / mass[None, :]
    return new_velocity, resultants, new_state
```

```python
import math

import jax
import jax.numpy as jnp
from jax import lax
from jax.sharding import PartitionSpec as P

TP = 8
NCLASS = 4
RES = 16
ITERS = 2
GHOST = 8


matrix_lame = 1.2
matrix_shear = 0.8
fiber_lame = 8.0
fiber_shear = 5.0
relax_rate = 1.0 / 288.0
time_step = 0.25


def with_halo(cells, sides, width):
    for axis, dim in sides:
        count = lax.axis_size(axis)
        head = lax.slice_in_dim(cells, 0, width, axis=dim)
        tail = lax.slice_in_dim(cells, cells.shape[dim] - width, cells.shape[dim], axis=dim)
        cells = jnp.concatenate(
            [
                lax.ppermute(tail, axis, [(i, (i + 1) % count) for i in range(count)]),
                cells,
                lax.ppermute(head, axis, [((i + 1) % count, i) for i in range(count)]),
            ],
            axis=dim,
        )
    return cells


def from_behind(value, axis, steps):
    count = lax.axis_size(axis)
    pairs = [(source, (source + steps) % count) for source in range(count)]
    return lax.ppermute(value, axis, pairs)


def material_stress(grads, lame_field, shear_field, macro):
    eps11 = macro[0] + grads[0][0]
    eps22 = macro[1] + grads[1][1]
    eps33 = grads[2][2]
    eps12 = macro[2] + 0.5 * (grads[0][1] + grads[1][0])
    eps13 = 0.5 * (grads[0][2] + grads[2][0])
    eps23 = 0.5 * (grads[1][2] + grads[2][1])
    volume = lame_field * (eps11 + eps22 + eps33)
    twice = 2.0 * shear_field
    return (
        volume + twice * eps11,
        volume + twice * eps22,
        volume + twice * eps33,
        twice * eps12,
        twice * eps13,
        twice * eps23,
    )


def rotate_in(strain, cosine, sine):
    first, second, shear = (strain[0], strain[1], strain[2])
    return jnp.stack(
        [
            cosine * cosine * first + sine * sine * second + 2.0 * cosine * sine * shear,
            sine * sine * first + cosine * cosine * second - 2.0 * cosine * sine * shear,
            -cosine * sine * first
            + cosine * sine * second
            + (cosine * cosine - sine * sine) * shear,
        ]
    )


def rotate_out(stress, cosine, sine):
    first, second, shear = (stress[0], stress[1], stress[2])
    return jnp.stack(
        [
            cosine * cosine * first + sine * sine * second - 2.0 * cosine * sine * shear,
            sine * sine * first + cosine * cosine * second + 2.0 * cosine * sine * shear,
            cosine * sine * first
            - cosine * sine * second
            + (cosine * cosine - sine * sine) * shear,
        ]
    )


def back_diff(field, axis):
    if axis == 0:
        return field[1:] - field[:-1]
    return (field - jnp.roll(field, 1, axis))[1:]


def relax_slab(displace, lame_field, shear_field, macro):
    front = displace[:, :-1]
    grads = [
        [
            displace[i, 1:] - front[i],
            jnp.roll(front[i], -1, 1) - front[i],
            jnp.roll(front[i], -1, 2) - front[i],
        ]
        for i in range(3)
    ]
    s11, s22, s33, s12, s13, s23 = material_stress(grads, lame_field, shear_field, macro)
    first = back_diff(s11, 0) + back_diff(s12, 1) + back_diff(s13, 2)
    second = back_diff(s12, 0) + back_diff(s22, 1) + back_diff(s23, 2)
    third = back_diff(s13, 0) + back_diff(s23, 1) + back_diff(s33, 2)
    shifted = displace[:, 1:-1] + relax_rate * jnp.stack([first, second, third])
    return (shifted, (s11, s22, s12))


def moduli_planes(phase_planes, class_hot):
    fiber_share = phase_planes[0].astype(jnp.float32)[..., None] * class_hot[0]
    for class_number in range(1, NCLASS):
        fiber_share = (
            fiber_share
            + phase_planes[class_number].astype(jnp.float32)[..., None] * class_hot[class_number]
        )
    lame_field = matrix_lame + (fiber_lame - matrix_lame) * fiber_share
    shear_field = matrix_shear + (fiber_shear - matrix_shear) * fiber_share
    return (lame_field, shear_field)


def shards(
    gen_strain, ply_class, route, phase, rve_state, connect, bmat, velocity, force_ext, mass
):
    highest = lax.Precision.HIGHEST
    thick_index = lax.axis_index("thick")
    per_group = route.shape[2]
    elements = gen_strain.shape[1]
    tile_count = lax.axis_size("tile")
    slab_count = lax.axis_size("rve")
    slots = rve_state.shape[4]
    capacity = slots // tile_count
    row_count = elements * per_group
    depth = ITERS
    up = [(i, (i + 1) % slab_count) for i in range(slab_count)]
    down = [((i + 1) % slab_count, i) for i in range(slab_count)]
    planes = rve_state.shape[1]
    below = lax.ppermute(rve_state[:, planes - depth :], "rve", up)
    above = lax.ppermute(rve_state[:, :depth], "rve", down)
    phase_below = lax.ppermute(phase[:, planes - depth :], "rve", up)
    phase_above = lax.ppermute(phase[:, :depth], "rve", down)
    layer = thick_index * per_group + jnp.arange(per_group, dtype=jnp.int32)
    heights = -1.0 + (2.0 * layer.astype(jnp.float32) + 1.0) / TP
    classes = lax.dynamic_slice_in_dim(ply_class, thick_index * per_group, per_group)
    angle = classes.astype(jnp.float32) * (math.pi / NCLASS)
    cosine = jnp.cos(angle)[None, :]
    sine = jnp.sin(angle)[None, :]
    membrane = gen_strain[:3][:, :, None]
    bending = gen_strain[3:][:, :, None]
    point_strain = membrane + heights[None, None, :] * bending
    rotated = rotate_in(point_strain, cosine, sine)
    row_class = jnp.broadcast_to(classes[None, :], (elements, per_group)).reshape(row_count)
    payload = jnp.concatenate(
        [rotated.reshape(3, row_count), row_class.astype(jnp.float32)[None, :]], 0
    ).T
    target = route.reshape(row_count)
    tile_hot = (target[:, None] == jnp.arange(tile_count, dtype=jnp.int32)[None, :]).astype(
        jnp.float32
    )
    row_ids = jnp.arange(row_count, dtype=jnp.int32)
    earlier_mask = (row_ids[:, None] > row_ids[None, :]).astype(jnp.float32)
    earlier = jnp.dot(earlier_mask, tile_hot, precision=highest)
    row_rank = jnp.sum(earlier * tile_hot, axis=1).astype(jnp.int32)
    slot_index = target * capacity + row_rank
    choose = (slot_index[:, None] == jnp.arange(slots, dtype=jnp.int32)[None, :]).astype(
        jnp.float32
    )
    send = jnp.dot(choose.T, payload, precision=highest)
    received = lax.all_to_all(
        send.reshape(tile_count, capacity, 4), "tile", split_axis=0, concat_axis=0, tiled=True
    ).reshape(slots, 4)
    macro = received[:, :3].T
    slot_class = received[:, 3].astype(jnp.int32)
    class_hot = (slot_class[None, :] == jnp.arange(NCLASS, dtype=jnp.int32)[:, None]).astype(
        jnp.float32
    )
    wide_phase = jnp.concatenate([phase_below, phase, phase_above], 1)
    lame_field, shear_field = moduli_planes(wide_phase, class_hot)
    displace = jnp.concatenate([below, rve_state, above], 1)
    stress = None
    for round_number in range(ITERS):
        count = displace.shape[1]
        displace, stress = relax_slab(
            displace,
            lame_field[round_number : round_number + count - 1],
            shear_field[round_number : round_number + count - 1],
            macro,
        )
    average = jnp.stack([jnp.sum(part[1:], axis=(0, 1, 2)) for part in stress]) / float(RES**3)
    returned = lax.all_to_all(
        average.T.reshape(tile_count, capacity, 3), "tile", split_axis=0, concat_axis=0, tiled=True
    )
    point_stress = jnp.dot(choose, returned.reshape(slots, 3), precision=highest)
    point_stress = point_stress.T.reshape(3, elements, per_group)
    global_stress = rotate_out(point_stress, cosine, sine)
    weight = 1.0 / TP
    forces = jnp.sum(global_stress, axis=2) * weight
    moments = jnp.sum(global_stress * heights[None, None, :], axis=2) * weight
    partial_terms = jnp.concatenate([forces, moments], 0)
    resultants = lax.psum(lax.psum(partial_terms, "rve"), "thick")
    corner_force = jnp.einsum("akme,me->ake", bmat, resultants, precision=highest)
    node_count = velocity.shape[1]
    node_hot = (
        connect[:, :, None] == jnp.arange(node_count + GHOST, dtype=jnp.int32)[None, None, :]
    ).astype(jnp.float32)
    assembled = jnp.einsum("ake,aen->kn", corner_force, node_hot, precision=highest)
    incoming = from_behind(assembled[:, node_count:], "tile", 1)
    internal = assembled[:, :node_count].at[:, :GHOST].add(incoming)
    new_velocity = velocity + time_step * (force_ext - internal) / mass[None, :]
    return (new_velocity, resultants, displace)


def solution(mesh):
    placed = (
        P(None, "tile"),
        P(),
        P("thick", "tile", None, None),
        P(None, "rve", None, None),
        P(None, "rve", None, None, ("tile", "thick")),
        P(None, "tile"),
        P(None, None, None, "tile"),
        P(None, "tile"),
        P(None, "tile"),
        P("tile"),
    )
    return jax.shard_map(
        shards,
        mesh=mesh,
        in_specs=placed,
        out_specs=(P(None, "tile"), P(None, "tile"), P(None, "rve", None, None, ("tile", "thick"))),
        check_vma=False,
    )
```

```python
import math

import jax
import jax.numpy as jnp
from jax import lax
from jax.sharding import PartitionSpec as P

TP = 8
NCLASS = 4
RES = 16
ITERS = 2
GHOST = 8


matrix_lame = 1.2
matrix_shear = 0.8
fiber_lame = 8.0
fiber_shear = 5.0
relax_rate = 1.0 / 288.0
time_step = 0.25


def with_halo(cells, sides, width):
    for axis, dim in sides:
        count = lax.axis_size(axis)
        head = lax.slice_in_dim(cells, 0, width, axis=dim)
        tail = lax.slice_in_dim(cells, cells.shape[dim] - width, cells.shape[dim], axis=dim)
        cells = jnp.concatenate(
            [
                lax.ppermute(tail, axis, [(i, (i + 1) % count) for i in range(count)]),
                cells,
                lax.ppermute(head, axis, [((i + 1) % count, i) for i in range(count)]),
            ],
            axis=dim,
        )
    return cells


def from_behind(value, axis, steps):
    count = lax.axis_size(axis)
    pairs = [(source, (source + steps) % count) for source in range(count)]
    return lax.ppermute(value, axis, pairs)


def material_stress(grads, lame_field, shear_field, macro):
    eps11 = macro[0] + grads[0][0]
    eps22 = macro[1] + grads[1][1]
    eps33 = grads[2][2]
    eps12 = macro[2] + 0.5 * (grads[0][1] + grads[1][0])
    eps13 = 0.5 * (grads[0][2] + grads[2][0])
    eps23 = 0.5 * (grads[1][2] + grads[2][1])
    volume = lame_field * (eps11 + eps22 + eps33)
    twice = 2.0 * shear_field
    return (
        volume + twice * eps11,
        volume + twice * eps22,
        volume + twice * eps33,
        twice * eps12,
        twice * eps13,
        twice * eps23,
    )


def rotate_in(strain, cosine, sine):
    first, second, shear = (strain[0], strain[1], strain[2])
    return jnp.stack(
        [
            cosine * cosine * first + sine * sine * second + 2.0 * cosine * sine * shear,
            sine * sine * first + cosine * cosine * second - 2.0 * cosine * sine * shear,
            -cosine * sine * first
            + cosine * sine * second
            + (cosine * cosine - sine * sine) * shear,
        ]
    )


def rotate_out(stress, cosine, sine):
    first, second, shear = (stress[0], stress[1], stress[2])
    return jnp.stack(
        [
            cosine * cosine * first + sine * sine * second - 2.0 * cosine * sine * shear,
            sine * sine * first + cosine * cosine * second + 2.0 * cosine * sine * shear,
            cosine * sine * first
            - cosine * sine * second
            + (cosine * cosine - sine * sine) * shear,
        ]
    )


def back_diff(field, axis):
    if axis == 0:
        return field[1:] - field[:-1]
    return (field - jnp.roll(field, 1, axis))[1:]


def relax_slab(displace, lame_field, shear_field, macro):
    front = displace[:, :-1]
    grads = [
        [
            displace[i, 1:] - front[i],
            jnp.roll(front[i], -1, 1) - front[i],
            jnp.roll(front[i], -1, 2) - front[i],
        ]
        for i in range(3)
    ]
    s11, s22, s33, s12, s13, s23 = material_stress(grads, lame_field, shear_field, macro)
    first = back_diff(s11, 0) + back_diff(s12, 1) + back_diff(s13, 2)
    second = back_diff(s12, 0) + back_diff(s22, 1) + back_diff(s23, 2)
    third = back_diff(s13, 0) + back_diff(s23, 1) + back_diff(s33, 2)
    shifted = displace[:, 1:-1] + relax_rate * jnp.stack([first, second, third])
    return (shifted, (s11, s22, s12))


def moduli_planes(phase_planes, class_hot):
    fiber_share = phase_planes[0].astype(jnp.float32)[..., None] * class_hot[0]
    for class_number in range(1, NCLASS):
        fiber_share = (
            fiber_share
            + phase_planes[class_number].astype(jnp.float32)[..., None] * class_hot[class_number]
        )
    lame_field = matrix_lame + (fiber_lame - matrix_lame) * fiber_share
    shear_field = matrix_shear + (fiber_shear - matrix_shear) * fiber_share
    return (lame_field, shear_field)


def slot_choice(target, tile_count, capacity, slots):
    highest = lax.Precision.HIGHEST
    row_count = target.shape[0]
    tile_hot = (target[:, None] == jnp.arange(tile_count, dtype=jnp.int32)[None, :]).astype(
        jnp.float32
    )
    row_ids = jnp.arange(row_count, dtype=jnp.int32)
    earlier_mask = (row_ids[:, None] > row_ids[None, :]).astype(jnp.float32)
    earlier = jnp.dot(earlier_mask, tile_hot, precision=highest)
    row_rank = jnp.sum(earlier * tile_hot, axis=1).astype(jnp.int32)
    slot_index = target * capacity + row_rank
    return (slot_index[:, None] == jnp.arange(slots, dtype=jnp.int32)[None, :]).astype(
        jnp.float32
    )


def tile_terms(choose, returned, cosine, sine, heights, elements, per_group):
    highest = lax.Precision.HIGHEST
    point_stress = jnp.dot(choose, returned, precision=highest)
    point_stress = point_stress.T.reshape(3, elements, per_group)
    global_stress = rotate_out(point_stress, cosine, sine)
    weight = 1.0 / TP
    forces = jnp.sum(global_stress, axis=2) * weight
    moments = jnp.sum(global_stress * heights[None, None, :], axis=2) * weight
    return jnp.concatenate([forces, moments], 0)


def node_forces(bmat, terms, connect, node_count):
    highest = lax.Precision.HIGHEST
    corner_force = jnp.einsum("akme,me->ake", bmat, terms, precision=highest)
    node_hot = (
        connect[:, :, None] == jnp.arange(node_count + GHOST, dtype=jnp.int32)[None, None, :]
    ).astype(jnp.float32)
    return jnp.einsum("ake,aen->kn", corner_force, node_hot, precision=highest)


def shards(
    gen_strain, ply_class, route, phase, rve_state, connect, bmat, velocity, force_ext, mass
):
    highest = lax.Precision.HIGHEST
    thick_index = lax.axis_index("thick")
    per_group = route.shape[2]
    elements = gen_strain.shape[1]
    tile_count = lax.axis_size("tile")
    slab_count = lax.axis_size("rve")
    slots = rve_state.shape[4]
    capacity = slots // tile_count
    row_count = elements * per_group
    depth = ITERS
    up = [(i, (i + 1) % slab_count) for i in range(slab_count)]
    down = [((i + 1) % slab_count, i) for i in range(slab_count)]
    planes = rve_state.shape[1]
    below = lax.ppermute(rve_state[:, planes - depth :], "rve", up)
    above = lax.ppermute(rve_state[:, :depth], "rve", down)
    phase_below = lax.ppermute(phase[:, planes - depth :], "rve", up)
    phase_above = lax.ppermute(phase[:, :depth], "rve", down)
    route_rows = route.reshape(elements, per_group).T
    prev_ints = from_behind(jnp.concatenate([route_rows, connect], 0), "tile", 1)
    prev_bmat = from_behind(bmat, "tile", 1)
    layer = thick_index * per_group + jnp.arange(per_group, dtype=jnp.int32)
    heights = -1.0 + (2.0 * layer.astype(jnp.float32) + 1.0) / TP
    classes = lax.dynamic_slice_in_dim(ply_class, thick_index * per_group, per_group)
    angle = classes.astype(jnp.float32) * (math.pi / NCLASS)
    cosine = jnp.cos(angle)[None, :]
    sine = jnp.sin(angle)[None, :]
    membrane = gen_strain[:3][:, :, None]
    bending = gen_strain[3:][:, :, None]
    point_strain = membrane + heights[None, None, :] * bending
    rotated = rotate_in(point_strain, cosine, sine)
    row_class = jnp.broadcast_to(classes[None, :], (elements, per_group)).reshape(row_count)
    payload = jnp.concatenate(
        [rotated.reshape(3, row_count), row_class.astype(jnp.float32)[None, :]], 0
    ).T
    choose = slot_choice(route.reshape(row_count), tile_count, capacity, slots)
    send = jnp.dot(choose.T, payload, precision=highest)
    received = lax.all_to_all(
        send.reshape(tile_count, capacity, 4), "tile", split_axis=0, concat_axis=0, tiled=True
    ).reshape(slots, 4)
    macro = received[:, :3].T
    slot_class = received[:, 3].astype(jnp.int32)
    class_hot = (slot_class[None, :] == jnp.arange(NCLASS, dtype=jnp.int32)[:, None]).astype(
        jnp.float32
    )
    wide_phase = jnp.concatenate([phase_below, phase, phase_above], 1)
    lame_field, shear_field = moduli_planes(wide_phase, class_hot)
    displace = jnp.concatenate([below, rve_state, above], 1)
    stress = None
    for round_number in range(ITERS):
        count = displace.shape[1]
        displace, stress = relax_slab(
            displace,
            lame_field[round_number : round_number + count - 1],
            shear_field[round_number : round_number + count - 1],
            macro,
        )
    average = jnp.stack([jnp.sum(part[1:], axis=(0, 1, 2)) for part in stress]) / float(RES**3)
    own_chunks = average.T.reshape(tile_count, capacity, 3)
    both_chunks = jnp.concatenate([own_chunks, jnp.roll(own_chunks, 1, axis=0)], 1)
    returned = lax.all_to_all(both_chunks, "tile", split_axis=0, concat_axis=0, tiled=True)
    own_returned = returned[:, :capacity].reshape(slots, 3)
    prev_returned = returned[:, capacity:].reshape(slots, 3)
    own_terms = tile_terms(choose, own_returned, cosine, sine, heights, elements, per_group)
    prev_route = prev_ints[:per_group].T.reshape(row_count)
    prev_connect = prev_ints[per_group:]
    prev_choose = slot_choice(prev_route, tile_count, capacity, slots)
    prev_terms = tile_terms(prev_choose, prev_returned, cosine, sine, heights, elements, per_group)
    node_count = velocity.shape[1]
    own_nodes = node_forces(bmat, own_terms, connect, node_count)[:, :node_count]
    ghost_nodes = node_forces(prev_bmat, prev_terms, prev_connect, node_count)[:, node_count:]
    partial_internal = own_nodes.at[:, :GHOST].add(ghost_nodes)
    totals = lax.psum(lax.psum(jnp.concatenate([own_terms, partial_internal], 0), "rve"), "thick")
    resultants = totals[:6]
    internal = totals[6:]
    new_velocity = velocity + time_step * (force_ext - internal) / mass[None, :]
    return (new_velocity, resultants, displace)


def solution(mesh):
    placed = (
        P(None, "tile"),
        P(),
        P("thick", "tile", None, None),
        P(None, "rve", None, None),
        P(None, "rve", None, None, ("tile", "thick")),
        P(None, "tile"),
        P(None, None, None, "tile"),
        P(None, "tile"),
        P(None, "tile"),
        P("tile"),
    )
    return jax.shard_map(
        shards,
        mesh=mesh,
        in_specs=placed,
        out_specs=(P(None, "tile"), P(None, "tile"), P(None, "rve", None, None, ("tile", "thick"))),
        check_vma=False,
    )
```

```python
import math

import jax
import jax.numpy as jnp
from jax import lax
from jax.sharding import PartitionSpec as P

TP = 8
NCLASS = 4
RES = 16
ITERS = 2
GHOST = 8


matrix_lame = 1.2
matrix_shear = 0.8
fiber_lame = 8.0
fiber_shear = 5.0
relax_rate = 1.0 / 288.0
time_step = 0.25


def with_halo(cells, sides, width):
    for axis, dim in sides:
        count = lax.axis_size(axis)
        head = lax.slice_in_dim(cells, 0, width, axis=dim)
        tail = lax.slice_in_dim(cells, cells.shape[dim] - width, cells.shape[dim], axis=dim)
        cells = jnp.concatenate(
            [
                lax.ppermute(tail, axis, [(i, (i + 1) % count) for i in range(count)]),
                cells,
                lax.ppermute(head, axis, [((i + 1) % count, i) for i in range(count)]),
            ],
            axis=dim,
        )
    return cells


def from_behind(value, axis, steps):
    count = lax.axis_size(axis)
    pairs = [(source, (source + steps) % count) for source in range(count)]
    return lax.ppermute(value, axis, pairs)


def material_stress(grads, lame_field, shear_field, macro):
    eps11 = macro[0] + grads[0][0]
    eps22 = macro[1] + grads[1][1]
    eps33 = grads[2][2]
    eps12 = macro[2] + 0.5 * (grads[0][1] + grads[1][0])
    eps13 = 0.5 * (grads[0][2] + grads[2][0])
    eps23 = 0.5 * (grads[1][2] + grads[2][1])
    volume = lame_field * (eps11 + eps22 + eps33)
    twice = 2.0 * shear_field
    return (
        volume + twice * eps11,
        volume + twice * eps22,
        volume + twice * eps33,
        twice * eps12,
        twice * eps13,
        twice * eps23,
    )


def rotate_in(strain, cosine, sine):
    first, second, shear = (strain[0], strain[1], strain[2])
    return jnp.stack(
        [
            cosine * cosine * first + sine * sine * second + 2.0 * cosine * sine * shear,
            sine * sine * first + cosine * cosine * second - 2.0 * cosine * sine * shear,
            -cosine * sine * first
            + cosine * sine * second
            + (cosine * cosine - sine * sine) * shear,
        ]
    )


def rotate_out(stress, cosine, sine):
    first, second, shear = (stress[0], stress[1], stress[2])
    return jnp.stack(
        [
            cosine * cosine * first + sine * sine * second - 2.0 * cosine * sine * shear,
            sine * sine * first + cosine * cosine * second + 2.0 * cosine * sine * shear,
            cosine * sine * first
            - cosine * sine * second
            + (cosine * cosine - sine * sine) * shear,
        ]
    )


def back_diff(field, axis):
    if axis == 0:
        return field[1:] - field[:-1]
    return (field - jnp.roll(field, 1, axis))[1:]


def relax_slab(displace, lame_field, shear_field, macro):
    front = displace[:, :-1]
    grads = [
        [
            displace[i, 1:] - front[i],
            jnp.roll(front[i], -1, 1) - front[i],
            jnp.roll(front[i], -1, 2) - front[i],
        ]
        for i in range(3)
    ]
    s11, s22, s33, s12, s13, s23 = material_stress(grads, lame_field, shear_field, macro)
    first = back_diff(s11, 0) + back_diff(s12, 1) + back_diff(s13, 2)
    second = back_diff(s12, 0) + back_diff(s22, 1) + back_diff(s23, 2)
    third = back_diff(s13, 0) + back_diff(s23, 1) + back_diff(s33, 2)
    shifted = displace[:, 1:-1] + relax_rate * jnp.stack([first, second, third])
    return (shifted, (s11, s22, s12))


def moduli_planes(phase_planes, class_hot):
    fiber_share = phase_planes[0].astype(jnp.float32)[..., None] * class_hot[0]
    for class_number in range(1, NCLASS):
        fiber_share = (
            fiber_share
            + phase_planes[class_number].astype(jnp.float32)[..., None] * class_hot[class_number]
        )
    lame_field = matrix_lame + (fiber_lame - matrix_lame) * fiber_share
    shear_field = matrix_shear + (fiber_shear - matrix_shear) * fiber_share
    return (lame_field, shear_field)


def slot_choice(target, tile_count, capacity, slots):
    highest = lax.Precision.HIGHEST
    row_count = target.shape[0]
    tile_hot = (target[:, None] == jnp.arange(tile_count, dtype=jnp.int32)[None, :]).astype(
        jnp.float32
    )
    row_ids = jnp.arange(row_count, dtype=jnp.int32)
    earlier_mask = (row_ids[:, None] > row_ids[None, :]).astype(jnp.float32)
    earlier = jnp.dot(earlier_mask, tile_hot, precision=highest)
    row_rank = jnp.sum(earlier * tile_hot, axis=1).astype(jnp.int32)
    slot_index = target * capacity + row_rank
    return (slot_index[:, None] == jnp.arange(slots, dtype=jnp.int32)[None, :]).astype(
        jnp.float32
    )


def tile_terms(choose, returned, cosine, sine, heights, elements, per_group):
    highest = lax.Precision.HIGHEST
    point_stress = jnp.dot(choose, returned, precision=highest)
    point_stress = point_stress.T.reshape(3, elements, per_group)
    global_stress = rotate_out(point_stress, cosine, sine)
    weight = 1.0 / TP
    forces = jnp.sum(global_stress, axis=2) * weight
    moments = jnp.sum(global_stress * heights[None, None, :], axis=2) * weight
    return jnp.concatenate([forces, moments], 0)


def node_forces(bmat, terms, connect, node_count):
    highest = lax.Precision.HIGHEST
    corner_force = jnp.einsum("akme,me->ake", bmat, terms, precision=highest)
    node_hot = (
        connect[:, :, None] == jnp.arange(node_count + GHOST, dtype=jnp.int32)[None, None, :]
    ).astype(jnp.float32)
    return jnp.einsum("ake,aen->kn", corner_force, node_hot, precision=highest)


def halo_pack(cells, phase_planes, pairs):
    lanes = cells.shape[-1]
    rows = cells.shape[-2]
    flat_cells = cells.reshape(-1, rows, lanes)
    flat_phase = phase_planes.astype(jnp.float32).reshape(-1, rows, lanes)
    moved = lax.ppermute(jnp.concatenate([flat_cells, flat_phase], 0), "rve", pairs)
    count = flat_cells.shape[0]
    cells_in = moved[:count].reshape(cells.shape)
    phase_in = moved[count:].reshape(phase_planes.shape).astype(jnp.int32)
    return (cells_in, phase_in)


def shards(
    gen_strain, ply_class, route, phase, rve_state, connect, bmat, velocity, force_ext, mass
):
    highest = lax.Precision.HIGHEST
    thick_index = lax.axis_index("thick")
    per_group = route.shape[2]
    elements = gen_strain.shape[1]
    tile_count = lax.axis_size("tile")
    slab_count = lax.axis_size("rve")
    slots = rve_state.shape[4]
    capacity = slots // tile_count
    row_count = elements * per_group
    depth = ITERS
    up = [(i, (i + 1) % slab_count) for i in range(slab_count)]
    down = [((i + 1) % slab_count, i) for i in range(slab_count)]
    planes = rve_state.shape[1]
    below, phase_below = halo_pack(rve_state[:, planes - depth :], phase[:, planes - depth :], up)
    above, phase_above = halo_pack(rve_state[:, :depth], phase[:, :depth], down)
    route_rows = route.reshape(elements, per_group).T
    int_rows = jnp.concatenate([route_rows, connect], 0)
    flat_bmat = bmat.reshape(-1, elements)
    prev_pack = from_behind(jnp.concatenate([flat_bmat, int_rows.astype(jnp.float32)], 0), "tile", 1)
    prev_bmat = prev_pack[: flat_bmat.shape[0]].reshape(bmat.shape)
    prev_ints = prev_pack[flat_bmat.shape[0] :].astype(jnp.int32)
    layer = thick_index * per_group + jnp.arange(per_group, dtype=jnp.int32)
    heights = -1.0 + (2.0 * layer.astype(jnp.float32) + 1.0) / TP
    classes = lax.dynamic_slice_in_dim(ply_class, thick_index * per_group, per_group)
    angle = classes.astype(jnp.float32) * (math.pi / NCLASS)
    cosine = jnp.cos(angle)[None, :]
    sine = jnp.sin(angle)[None, :]
    membrane = gen_strain[:3][:, :, None]
    bending = gen_strain[3:][:, :, None]
    point_strain = membrane + heights[None, None, :] * bending
    rotated = rotate_in(point_strain, cosine, sine)
    row_class = jnp.broadcast_to(classes[None, :], (elements, per_group)).reshape(row_count)
    payload = jnp.concatenate(
        [rotated.reshape(3, row_count), row_class.astype(jnp.float32)[None, :]], 0
    ).T
    choose = slot_choice(route.reshape(row_count), tile_count, capacity, slots)
    send = jnp.dot(choose.T, payload, precision=highest)
    received = lax.all_to_all(
        send.reshape(tile_count, capacity, 4), "tile", split_axis=0, concat_axis=0, tiled=True
    ).reshape(slots, 4)
    macro = received[:, :3].T
    slot_class = received[:, 3].astype(jnp.int32)
    class_hot = (slot_class[None, :] == jnp.arange(NCLASS, dtype=jnp.int32)[:, None]).astype(
        jnp.float32
    )
    wide_phase = jnp.concatenate([phase_below, phase, phase_above], 1)
    lame_field, shear_field = moduli_planes(wide_phase, class_hot)
    displace = jnp.concatenate([below, rve_state, above], 1)
    stress = None
    for round_number in range(ITERS):
        count = displace.shape[1]
        displace, stress = relax_slab(
            displace,
            lame_field[round_number : round_number + count - 1],
            shear_field[round_number : round_number + count - 1],
            macro,
        )
    average = jnp.stack([jnp.sum(part[1:], axis=(0, 1, 2)) for part in stress]) / float(RES**3)
    own_chunks = average.T.reshape(tile_count, capacity, 3)
    both_chunks = jnp.concatenate([own_chunks, jnp.roll(own_chunks, 1, axis=0)], 1)
    returned = lax.all_to_all(both_chunks, "tile", split_axis=0, concat_axis=0, tiled=True)
    own_returned = returned[:, :capacity].reshape(slots, 3)
    prev_returned = returned[:, capacity:].reshape(slots, 3)
    own_terms = tile_terms(choose, own_returned, cosine, sine, heights, elements, per_group)
    prev_route = prev_ints[:per_group].T.reshape(row_count)
    prev_connect = prev_ints[per_group:]
    prev_choose = slot_choice(prev_route, tile_count, capacity, slots)
    prev_terms = tile_terms(prev_choose, prev_returned, cosine, sine, heights, elements, per_group)
    node_count = velocity.shape[1]
    own_nodes = node_forces(bmat, own_terms, connect, node_count)[:, :node_count]
    ghost_nodes = node_forces(prev_bmat, prev_terms, prev_connect, node_count)[:, node_count:]
    partial_internal = own_nodes.at[:, :GHOST].add(ghost_nodes)
    totals = lax.psum(lax.psum(jnp.concatenate([own_terms, partial_internal], 0), "rve"), "thick")
    resultants = totals[:6]
    internal = totals[6:]
    new_velocity = velocity + time_step * (force_ext - internal) / mass[None, :]
    return (new_velocity, resultants, displace)


def solution(mesh):
    placed = (
        P(None, "tile"),
        P(),
        P("thick", "tile", None, None),
        P(None, "rve", None, None),
        P(None, "rve", None, None, ("tile", "thick")),
        P(None, "tile"),
        P(None, None, None, "tile"),
        P(None, "tile"),
        P(None, "tile"),
        P("tile"),
    )
    return jax.shard_map(
        shards,
        mesh=mesh,
        in_specs=placed,
        out_specs=(P(None, "tile"), P(None, "tile"), P(None, "rve", None, None, ("tile", "thick"))),
        check_vma=False,
    )
```

```python
import math

import jax
import jax.numpy as jnp
from jax import lax
from jax.experimental import pallas as pl
from jax.experimental.pallas import tpu as pltpu
from jax.sharding import PartitionSpec as P

TP = 8
NCLASS = 4
RES = 16
ITERS = 2
GHOST = 8


matrix_lame = 1.2
matrix_shear = 0.8
fiber_lame = 8.0
fiber_shear = 5.0
relax_rate = 1.0 / 288.0
time_step = 0.25


def with_halo(cells, sides, width):
    for axis, dim in sides:
        count = lax.axis_size(axis)
        head = lax.slice_in_dim(cells, 0, width, axis=dim)
        tail = lax.slice_in_dim(cells, cells.shape[dim] - width, cells.shape[dim], axis=dim)
        cells = jnp.concatenate(
            [
                lax.ppermute(tail, axis, [(i, (i + 1) % count) for i in range(count)]),
                cells,
                lax.ppermute(head, axis, [((i + 1) % count, i) for i in range(count)]),
            ],
            axis=dim,
        )
    return cells


def from_behind(value, axis, steps):
    count = lax.axis_size(axis)
    pairs = [(source, (source + steps) % count) for source in range(count)]
    return lax.ppermute(value, axis, pairs)


def material_stress(grads, lame_field, shear_field, macro):
    eps11 = macro[0] + grads[0][0]
    eps22 = macro[1] + grads[1][1]
    eps33 = grads[2][2]
    eps12 = macro[2] + 0.5 * (grads[0][1] + grads[1][0])
    eps13 = 0.5 * (grads[0][2] + grads[2][0])
    eps23 = 0.5 * (grads[1][2] + grads[2][1])
    volume = lame_field * (eps11 + eps22 + eps33)
    twice = 2.0 * shear_field
    return (
        volume + twice * eps11,
        volume + twice * eps22,
        volume + twice * eps33,
        twice * eps12,
        twice * eps13,
        twice * eps23,
    )


def rotate_in(strain, cosine, sine):
    first, second, shear = (strain[0], strain[1], strain[2])
    return jnp.stack(
        [
            cosine * cosine * first + sine * sine * second + 2.0 * cosine * sine * shear,
            sine * sine * first + cosine * cosine * second - 2.0 * cosine * sine * shear,
            -cosine * sine * first
            + cosine * sine * second
            + (cosine * cosine - sine * sine) * shear,
        ]
    )


def rotate_out(stress, cosine, sine):
    first, second, shear = (stress[0], stress[1], stress[2])
    return jnp.stack(
        [
            cosine * cosine * first + sine * sine * second - 2.0 * cosine * sine * shear,
            sine * sine * first + cosine * cosine * second + 2.0 * cosine * sine * shear,
            cosine * sine * first
            - cosine * sine * second
            + (cosine * cosine - sine * sine) * shear,
        ]
    )


def back_diff(field, axis):
    if axis == 0:
        return field[1:] - field[:-1]
    return (field - jnp.roll(field, 1, axis))[1:]


def relax_slab(displace, lame_field, shear_field, macro):
    front = displace[:, :-1]
    grads = [
        [
            displace[i, 1:] - front[i],
            jnp.roll(front[i], -1, 1) - front[i],
            jnp.roll(front[i], -1, 2) - front[i],
        ]
        for i in range(3)
    ]
    s11, s22, s33, s12, s13, s23 = material_stress(grads, lame_field, shear_field, macro)
    first = back_diff(s11, 0) + back_diff(s12, 1) + back_diff(s13, 2)
    second = back_diff(s12, 0) + back_diff(s22, 1) + back_diff(s23, 2)
    third = back_diff(s13, 0) + back_diff(s23, 1) + back_diff(s33, 2)
    shifted = displace[:, 1:-1] + relax_rate * jnp.stack([first, second, third])
    return (shifted, (s11, s22, s12))


def moduli_planes(phase_planes, class_hot):
    fiber_share = phase_planes[0].astype(jnp.float32)[..., None] * class_hot[0]
    for class_number in range(1, NCLASS):
        fiber_share = (
            fiber_share
            + phase_planes[class_number].astype(jnp.float32)[..., None] * class_hot[class_number]
        )
    lame_field = matrix_lame + (fiber_lame - matrix_lame) * fiber_share
    shear_field = matrix_shear + (fiber_shear - matrix_shear) * fiber_share
    return (lame_field, shear_field)


def slot_choice(target, tile_count, capacity, slots):
    highest = lax.Precision.HIGHEST
    row_count = target.shape[0]
    tile_hot = (target[:, None] == jnp.arange(tile_count, dtype=jnp.int32)[None, :]).astype(
        jnp.float32
    )
    row_ids = jnp.arange(row_count, dtype=jnp.int32)
    earlier_mask = (row_ids[:, None] > row_ids[None, :]).astype(jnp.float32)
    earlier = jnp.dot(earlier_mask, tile_hot, precision=highest)
    row_rank = jnp.sum(earlier * tile_hot, axis=1).astype(jnp.int32)
    slot_index = target * capacity + row_rank
    return (slot_index[:, None] == jnp.arange(slots, dtype=jnp.int32)[None, :]).astype(
        jnp.float32
    )


def tile_terms(choose, returned, cosine, sine, heights, elements, per_group):
    highest = lax.Precision.HIGHEST
    point_stress = jnp.dot(choose, returned, precision=highest)
    point_stress = point_stress.T.reshape(3, elements, per_group)
    global_stress = rotate_out(point_stress, cosine, sine)
    weight = 1.0 / TP
    forces = jnp.sum(global_stress, axis=2) * weight
    moments = jnp.sum(global_stress * heights[None, None, :], axis=2) * weight
    return jnp.concatenate([forces, moments], 0)


def node_forces(bmat, terms, connect, node_count):
    highest = lax.Precision.HIGHEST
    corner_force = jnp.einsum("akme,me->ake", bmat, terms, precision=highest)
    node_hot = (
        connect[:, :, None] == jnp.arange(node_count + GHOST, dtype=jnp.int32)[None, None, :]
    ).astype(jnp.float32)
    return jnp.einsum("ake,aen->kn", corner_force, node_hot, precision=highest)


def shift_rows(field, shift, axis):
    if axis == 1:
        size = field.shape[1]
        cut = (size - shift) % size
        return jnp.concatenate([field[:, cut:], field[:, :cut]], 1)
    return pltpu.roll(field, shift % field.shape[axis], axis)


def kernel_sweep(cells, lame_field, shear_field, macro):
    front = [part[:-1] for part in cells]
    grads = [
        [
            cells[i][1:] - front[i],
            shift_rows(front[i], -1, 1) - front[i],
            shift_rows(front[i], -1, 2) - front[i],
        ]
        for i in range(3)
    ]
    s11, s22, s33, s12, s13, s23 = material_stress(grads, lame_field, shear_field, macro)

    def diff(field, axis):
        if axis == 0:
            return field[1:] - field[:-1]
        return (field - shift_rows(field, 1, axis))[1:]

    first = diff(s11, 0) + diff(s12, 1) + diff(s13, 2)
    second = diff(s12, 0) + diff(s22, 1) + diff(s23, 2)
    third = diff(s13, 0) + diff(s23, 1) + diff(s33, 2)
    moved = [
        cells[i][1:-1] + relax_rate * rate_term
        for i, rate_term in enumerate((first, second, third))
    ]
    return (moved, (s11, s22, s12))


def relax_kernel(cells_ref, lame_ref, shear_ref, macro_ref, out_ref, mean_ref):
    cells = [cells_ref[i] for i in range(3)]
    lame_all = lame_ref[...]
    shear_all = shear_ref[...]
    macro = [macro_ref[k : k + 1, :].reshape(1, 1, 1, -1) for k in range(3)]
    stress = None
    for round_number in range(ITERS):
        count = cells[0].shape[0]
        cells, stress = kernel_sweep(
            cells,
            lame_all[round_number : round_number + count - 1],
            shear_all[round_number : round_number + count - 1],
            macro,
        )
    for i in range(3):
        out_ref[i] = cells[i]
    for k in range(3):
        total = jnp.sum(stress[k][1:], axis=(0, 1))
        mean_ref[k : k + 1, :] = jnp.sum(total, axis=0, keepdims=True) / float(RES**3)


def relax_slab_kernel(displace, lame_field, shear_field, macro):
    planes = displace.shape[1] - 2 * ITERS
    out_shape = (
        jax.ShapeDtypeStruct((3, planes) + displace.shape[2:], jnp.float32),
        jax.ShapeDtypeStruct((3, displace.shape[-1]), jnp.float32),
    )
    return pl.pallas_call(
        relax_kernel,
        out_shape=out_shape,
        in_specs=[pl.BlockSpec(memory_space=pltpu.VMEM)] * 4,
        out_specs=(pl.BlockSpec(memory_space=pltpu.VMEM), pl.BlockSpec(memory_space=pltpu.VMEM)),
        compiler_params=pltpu.CompilerParams(vmem_limit_bytes=60 * 1024 * 1024),
    )(displace, lame_field, shear_field, macro)


def shards(
    gen_strain, ply_class, route, phase, rve_state, connect, bmat, velocity, force_ext, mass
):
    highest = lax.Precision.HIGHEST
    thick_index = lax.axis_index("thick")
    per_group = route.shape[2]
    elements = gen_strain.shape[1]
    tile_count = lax.axis_size("tile")
    slab_count = lax.axis_size("rve")
    slots = rve_state.shape[4]
    capacity = slots // tile_count
    row_count = elements * per_group
    depth = ITERS
    up = [(i, (i + 1) % slab_count) for i in range(slab_count)]
    down = [((i + 1) % slab_count, i) for i in range(slab_count)]
    planes = rve_state.shape[1]
    below = lax.ppermute(rve_state[:, planes - depth :], "rve", up)
    above = lax.ppermute(rve_state[:, :depth], "rve", down)
    phase_below = lax.ppermute(phase[:, planes - depth :], "rve", up)
    phase_above = lax.ppermute(phase[:, :depth], "rve", down)
    route_rows = route.reshape(elements, per_group).T
    prev_ints = from_behind(jnp.concatenate([route_rows, connect], 0), "tile", 1)
    prev_bmat = from_behind(bmat, "tile", 1)
    layer = thick_index * per_group + jnp.arange(per_group, dtype=jnp.int32)
    heights = -1.0 + (2.0 * layer.astype(jnp.float32) + 1.0) / TP
    classes = lax.dynamic_slice_in_dim(ply_class, thick_index * per_group, per_group)
    angle = classes.astype(jnp.float32) * (math.pi / NCLASS)
    cosine = jnp.cos(angle)[None, :]
    sine = jnp.sin(angle)[None, :]
    membrane = gen_strain[:3][:, :, None]
    bending = gen_strain[3:][:, :, None]
    point_strain = membrane + heights[None, None, :] * bending
    rotated = rotate_in(point_strain, cosine, sine)
    row_class = jnp.broadcast_to(classes[None, :], (elements, per_group)).reshape(row_count)
    payload = jnp.concatenate(
        [rotated.reshape(3, row_count), row_class.astype(jnp.float32)[None, :]], 0
    ).T
    choose = slot_choice(route.reshape(row_count), tile_count, capacity, slots)
    send = jnp.dot(choose.T, payload, precision=highest)
    received = lax.all_to_all(
        send.reshape(tile_count, capacity, 4), "tile", split_axis=0, concat_axis=0, tiled=True
    ).reshape(slots, 4)
    macro = received[:, :3].T
    slot_class = received[:, 3].astype(jnp.int32)
    class_hot = (slot_class[None, :] == jnp.arange(NCLASS, dtype=jnp.int32)[:, None]).astype(
        jnp.float32
    )
    wide_phase = jnp.concatenate([phase_below, phase, phase_above], 1)
    lame_field, shear_field = moduli_planes(wide_phase, class_hot)
    displace = jnp.concatenate([below, rve_state, above], 1)
    displace, average = relax_slab_kernel(displace, lame_field, shear_field, macro)
    own_chunks = average.T.reshape(tile_count, capacity, 3)
    both_chunks = jnp.concatenate([own_chunks, jnp.roll(own_chunks, 1, axis=0)], 1)
    returned = lax.all_to_all(both_chunks, "tile", split_axis=0, concat_axis=0, tiled=True)
    own_returned = returned[:, :capacity].reshape(slots, 3)
    prev_returned = returned[:, capacity:].reshape(slots, 3)
    own_terms = tile_terms(choose, own_returned, cosine, sine, heights, elements, per_group)
    prev_route = prev_ints[:per_group].T.reshape(row_count)
    prev_connect = prev_ints[per_group:]
    prev_choose = slot_choice(prev_route, tile_count, capacity, slots)
    prev_terms = tile_terms(prev_choose, prev_returned, cosine, sine, heights, elements, per_group)
    node_count = velocity.shape[1]
    own_nodes = node_forces(bmat, own_terms, connect, node_count)[:, :node_count]
    ghost_nodes = node_forces(prev_bmat, prev_terms, prev_connect, node_count)[:, node_count:]
    partial_internal = own_nodes.at[:, :GHOST].add(ghost_nodes)
    totals = lax.psum(lax.psum(jnp.concatenate([own_terms, partial_internal], 0), "rve"), "thick")
    resultants = totals[:6]
    internal = totals[6:]
    new_velocity = velocity + time_step * (force_ext - internal) / mass[None, :]
    return (new_velocity, resultants, displace)


def solution(mesh):
    placed = (
        P(None, "tile"),
        P(),
        P("thick", "tile", None, None),
        P(None, "rve", None, None),
        P(None, "rve", None, None, ("tile", "thick")),
        P(None, "tile"),
        P(None, None, None, "tile"),
        P(None, "tile"),
        P(None, "tile"),
        P("tile"),
    )
    return jax.shard_map(
        shards,
        mesh=mesh,
        in_specs=placed,
        out_specs=(P(None, "tile"), P(None, "tile"), P(None, "rve", None, None, ("tile", "thick"))),
        check_vma=False,
    )
```

```python
import math

import jax
import jax.numpy as jnp
from jax import lax
from jax.experimental import pallas as pl
from jax.experimental.pallas import tpu as pltpu
from jax.sharding import PartitionSpec as P

TP = 8
NCLASS = 4
RES = 16
ITERS = 2
GHOST = 8


matrix_lame = 1.2
matrix_shear = 0.8
fiber_lame = 8.0
fiber_shear = 5.0
relax_rate = 1.0 / 288.0
time_step = 0.25


def with_halo(cells, sides, width):
    for axis, dim in sides:
        count = lax.axis_size(axis)
        head = lax.slice_in_dim(cells, 0, width, axis=dim)
        tail = lax.slice_in_dim(cells, cells.shape[dim] - width, cells.shape[dim], axis=dim)
        cells = jnp.concatenate(
            [
                lax.ppermute(tail, axis, [(i, (i + 1) % count) for i in range(count)]),
                cells,
                lax.ppermute(head, axis, [((i + 1) % count, i) for i in range(count)]),
            ],
            axis=dim,
        )
    return cells


def from_behind(value, axis, steps):
    count = lax.axis_size(axis)
    pairs = [(source, (source + steps) % count) for source in range(count)]
    return lax.ppermute(value, axis, pairs)


def material_stress(grads, lame_field, shear_field, macro):
    eps11 = macro[0] + grads[0][0]
    eps22 = macro[1] + grads[1][1]
    eps33 = grads[2][2]
    eps12 = macro[2] + 0.5 * (grads[0][1] + grads[1][0])
    eps13 = 0.5 * (grads[0][2] + grads[2][0])
    eps23 = 0.5 * (grads[1][2] + grads[2][1])
    volume = lame_field * (eps11 + eps22 + eps33)
    twice = 2.0 * shear_field
    return (
        volume + twice * eps11,
        volume + twice * eps22,
        volume + twice * eps33,
        twice * eps12,
        twice * eps13,
        twice * eps23,
    )


def rotate_in(strain, cosine, sine):
    first, second, shear = (strain[0], strain[1], strain[2])
    return jnp.stack(
        [
            cosine * cosine * first + sine * sine * second + 2.0 * cosine * sine * shear,
            sine * sine * first + cosine * cosine * second - 2.0 * cosine * sine * shear,
            -cosine * sine * first
            + cosine * sine * second
            + (cosine * cosine - sine * sine) * shear,
        ]
    )


def rotate_out(stress, cosine, sine):
    first, second, shear = (stress[0], stress[1], stress[2])
    return jnp.stack(
        [
            cosine * cosine * first + sine * sine * second - 2.0 * cosine * sine * shear,
            sine * sine * first + cosine * cosine * second + 2.0 * cosine * sine * shear,
            cosine * sine * first
            - cosine * sine * second
            + (cosine * cosine - sine * sine) * shear,
        ]
    )


def back_diff(field, axis):
    if axis == 0:
        return field[1:] - field[:-1]
    return (field - jnp.roll(field, 1, axis))[1:]


def relax_slab(displace, lame_field, shear_field, macro):
    front = displace[:, :-1]
    grads = [
        [
            displace[i, 1:] - front[i],
            jnp.roll(front[i], -1, 1) - front[i],
            jnp.roll(front[i], -1, 2) - front[i],
        ]
        for i in range(3)
    ]
    s11, s22, s33, s12, s13, s23 = material_stress(grads, lame_field, shear_field, macro)
    first = back_diff(s11, 0) + back_diff(s12, 1) + back_diff(s13, 2)
    second = back_diff(s12, 0) + back_diff(s22, 1) + back_diff(s23, 2)
    third = back_diff(s13, 0) + back_diff(s23, 1) + back_diff(s33, 2)
    shifted = displace[:, 1:-1] + relax_rate * jnp.stack([first, second, third])
    return (shifted, (s11, s22, s12))


def moduli_planes(phase_planes, class_hot):
    fiber_share = phase_planes[0].astype(jnp.float32)[..., None] * class_hot[0]
    for class_number in range(1, NCLASS):
        fiber_share = (
            fiber_share
            + phase_planes[class_number].astype(jnp.float32)[..., None] * class_hot[class_number]
        )
    lame_field = matrix_lame + (fiber_lame - matrix_lame) * fiber_share
    shear_field = matrix_shear + (fiber_shear - matrix_shear) * fiber_share
    return (lame_field, shear_field)


def slot_choice(target, tile_count, capacity, slots):
    highest = lax.Precision.HIGHEST
    row_count = target.shape[0]
    tile_hot = (target[:, None] == jnp.arange(tile_count, dtype=jnp.int32)[None, :]).astype(
        jnp.float32
    )
    row_ids = jnp.arange(row_count, dtype=jnp.int32)
    earlier_mask = (row_ids[:, None] > row_ids[None, :]).astype(jnp.float32)
    earlier = jnp.dot(earlier_mask, tile_hot, precision=highest)
    row_rank = jnp.sum(earlier * tile_hot, axis=1).astype(jnp.int32)
    slot_index = target * capacity + row_rank
    return (slot_index[:, None] == jnp.arange(slots, dtype=jnp.int32)[None, :]).astype(
        jnp.float32
    )


def tile_terms(choose, returned, cosine, sine, heights, elements, per_group):
    highest = lax.Precision.HIGHEST
    point_stress = jnp.dot(choose, returned, precision=highest)
    point_stress = point_stress.T.reshape(3, elements, per_group)
    global_stress = rotate_out(point_stress, cosine, sine)
    weight = 1.0 / TP
    forces = jnp.sum(global_stress, axis=2) * weight
    moments = jnp.sum(global_stress * heights[None, None, :], axis=2) * weight
    return jnp.concatenate([forces, moments], 0)


def node_forces(bmat, terms, connect, node_count):
    highest = lax.Precision.HIGHEST
    corner_force = jnp.einsum("akme,me->ake", bmat, terms, precision=highest)
    node_hot = (
        connect[:, :, None] == jnp.arange(node_count + GHOST, dtype=jnp.int32)[None, None, :]
    ).astype(jnp.float32)
    return jnp.einsum("ake,aen->kn", corner_force, node_hot, precision=highest)


def shift_rows(field, shift, axis):
    if axis == 1:
        size = field.shape[1]
        cut = (size - shift) % size
        return jnp.concatenate([field[:, cut:], field[:, :cut]], 1)
    return pltpu.roll(field, shift % field.shape[axis], axis)


def kernel_sweep(cells, lame_field, shear_field, macro):
    front = [part[:-1] for part in cells]
    grads = [
        [
            cells[i][1:] - front[i],
            shift_rows(front[i], -1, 1) - front[i],
            shift_rows(front[i], -1, 2) - front[i],
        ]
        for i in range(3)
    ]
    s11, s22, s33, s12, s13, s23 = material_stress(grads, lame_field, shear_field, macro)

    def diff(field, axis):
        if axis == 0:
            return field[1:] - field[:-1]
        return (field - shift_rows(field, 1, axis))[1:]

    first = diff(s11, 0) + diff(s12, 1) + diff(s13, 2)
    second = diff(s12, 0) + diff(s22, 1) + diff(s23, 2)
    third = diff(s13, 0) + diff(s23, 1) + diff(s33, 2)
    moved = [
        cells[i][1:-1] + relax_rate * rate_term
        for i, rate_term in enumerate((first, second, third))
    ]
    return (moved, (s11, s22, s12))


def relax_kernel(low_ref, state_ref, high_ref, lame_ref, shear_ref, macro_ref, out_ref, mean_ref):
    rows = state_ref.shape[2]
    depth = ITERS

    def halo_planes(ref, component):
        return [
            ref[pl.ds((component * depth + p) * rows, rows)][None] for p in range(depth)
        ]

    cells = [
        jnp.concatenate(
            halo_planes(low_ref, i) + [state_ref[i]] + halo_planes(high_ref, i), 0
        )
        for i in range(3)
    ]
    lame_all = lame_ref[...]
    shear_all = shear_ref[...]
    macro = [macro_ref[k : k + 1, :].reshape(1, 1, 1, -1) for k in range(3)]
    stress = None
    for round_number in range(ITERS):
        count = cells[0].shape[0]
        cells, stress = kernel_sweep(
            cells,
            lame_all[round_number : round_number + count - 1],
            shear_all[round_number : round_number + count - 1],
            macro,
        )
    for i in range(3):
        out_ref[i] = cells[i]
    for k in range(3):
        total = jnp.sum(stress[k][1:], axis=(0, 1))
        mean_ref[k : k + 1, :] = jnp.sum(total, axis=0, keepdims=True) / float(RES**3)


def relax_slab_kernel(low, state, high, lame_field, shear_field, macro):
    out_shape = (
        jax.ShapeDtypeStruct(state.shape, jnp.float32),
        jax.ShapeDtypeStruct((3, state.shape[-1]), jnp.float32),
    )
    return pl.pallas_call(
        relax_kernel,
        out_shape=out_shape,
        in_specs=[pl.BlockSpec(memory_space=pltpu.VMEM)] * 6,
        out_specs=(pl.BlockSpec(memory_space=pltpu.VMEM), pl.BlockSpec(memory_space=pltpu.VMEM)),
        compiler_params=pltpu.CompilerParams(vmem_limit_bytes=60 * 1024 * 1024),
    )(low, state, high, lame_field, shear_field, macro)


def halo_pack(cells, phase_planes, pairs):
    lanes = cells.shape[-1]
    rows = cells.shape[-2]
    flat_cells = cells.reshape(-1, rows, lanes)
    flat_phase = phase_planes.astype(jnp.float32).reshape(-1, rows, lanes)
    moved = lax.ppermute(jnp.concatenate([flat_cells, flat_phase], 0), "rve", pairs)
    phase_in = moved[flat_cells.shape[0] :].reshape(phase_planes.shape).astype(jnp.int32)
    return (moved, phase_in)


def shards(
    gen_strain, ply_class, route, phase, rve_state, connect, bmat, velocity, force_ext, mass
):
    highest = lax.Precision.HIGHEST
    thick_index = lax.axis_index("thick")
    per_group = route.shape[2]
    elements = gen_strain.shape[1]
    tile_count = lax.axis_size("tile")
    slab_count = lax.axis_size("rve")
    slots = rve_state.shape[4]
    capacity = slots // tile_count
    row_count = elements * per_group
    depth = ITERS
    up = [(i, (i + 1) % slab_count) for i in range(slab_count)]
    down = [((i + 1) % slab_count, i) for i in range(slab_count)]
    planes = rve_state.shape[1]
    below, phase_below = halo_pack(rve_state[:, planes - depth :], phase[:, planes - depth :], up)
    above, phase_above = halo_pack(rve_state[:, :depth], phase[:, :depth], down)
    layer = thick_index * per_group + jnp.arange(per_group, dtype=jnp.int32)
    heights = -1.0 + (2.0 * layer.astype(jnp.float32) + 1.0) / TP
    classes = lax.dynamic_slice_in_dim(ply_class, thick_index * per_group, per_group)
    angle = classes.astype(jnp.float32) * (math.pi / NCLASS)
    cosine = jnp.cos(angle)[None, :]
    sine = jnp.sin(angle)[None, :]
    membrane = gen_strain[:3][:, :, None]
    bending = gen_strain[3:][:, :, None]
    point_strain = membrane + heights[None, None, :] * bending
    rotated = rotate_in(point_strain, cosine, sine)
    row_class = jnp.broadcast_to(classes[None, :], (elements, per_group)).reshape(row_count)
    payload = jnp.concatenate(
        [rotated.reshape(3, row_count), row_class.astype(jnp.float32)[None, :]], 0
    ).T
    choose = slot_choice(route.reshape(row_count), tile_count, capacity, slots)
    send = jnp.dot(choose.T, payload, precision=highest)
    received = lax.all_to_all(
        send.reshape(tile_count, capacity, 4), "tile", split_axis=0, concat_axis=0, tiled=True
    ).reshape(slots, 4)
    macro = received[:, :3].T
    slot_class = received[:, 3].astype(jnp.int32)
    class_hot = (slot_class[None, :] == jnp.arange(NCLASS, dtype=jnp.int32)[:, None]).astype(
        jnp.float32
    )
    wide_phase = jnp.concatenate([phase_below, phase, phase_above], 1)
    lame_field, shear_field = moduli_planes(wide_phase, class_hot)
    displace, average = relax_slab_kernel(below, rve_state, above, lame_field, shear_field, macro)
    returned = lax.all_to_all(
        average.T.reshape(tile_count, capacity, 3), "tile", split_axis=0, concat_axis=0, tiled=True
    )
    own_terms = tile_terms(choose, returned.reshape(slots, 3), cosine, sine, heights, elements, per_group)
    resultants = lax.psum(lax.psum(own_terms, "rve"), "thick")
    node_count = velocity.shape[1]
    assembled = node_forces(bmat, resultants, connect, node_count)
    incoming = from_behind(assembled[:, node_count:], "tile", 1)
    internal = assembled[:, :node_count].at[:, :GHOST].add(incoming)
    new_velocity = velocity + time_step * (force_ext - internal) / mass[None, :]
    return (new_velocity, resultants, displace)


def solution(mesh):
    placed = (
        P(None, "tile"),
        P(),
        P("thick", "tile", None, None),
        P(None, "rve", None, None),
        P(None, "rve", None, None, ("tile", "thick")),
        P(None, "tile"),
        P(None, None, None, "tile"),
        P(None, "tile"),
        P(None, "tile"),
        P("tile"),
    )
    return jax.shard_map(
        shards,
        mesh=mesh,
        in_specs=placed,
        out_specs=(P(None, "tile"), P(None, "tile"), P(None, "rve", None, None, ("tile", "thick"))),
        check_vma=False,
    )
```

```python
import math

import jax
import jax.numpy as jnp
from jax import lax
from jax.experimental import pallas as pl
from jax.experimental.pallas import tpu as pltpu
from jax.sharding import PartitionSpec as P

TP = 8
NCLASS = 4
RES = 16
ITERS = 2
GHOST = 8


matrix_lame = 1.2
matrix_shear = 0.8
fiber_lame = 8.0
fiber_shear = 5.0
relax_rate = 1.0 / 288.0
time_step = 0.25


def with_halo(cells, sides, width):
    for axis, dim in sides:
        count = lax.axis_size(axis)
        head = lax.slice_in_dim(cells, 0, width, axis=dim)
        tail = lax.slice_in_dim(cells, cells.shape[dim] - width, cells.shape[dim], axis=dim)
        cells = jnp.concatenate(
            [
                lax.ppermute(tail, axis, [(i, (i + 1) % count) for i in range(count)]),
                cells,
                lax.ppermute(head, axis, [((i + 1) % count, i) for i in range(count)]),
            ],
            axis=dim,
        )
    return cells


def from_behind(value, axis, steps):
    count = lax.axis_size(axis)
    pairs = [(source, (source + steps) % count) for source in range(count)]
    return lax.ppermute(value, axis, pairs)


def material_stress(grads, lame_field, shear_field, macro):
    eps11 = macro[0] + grads[0][0]
    eps22 = macro[1] + grads[1][1]
    eps33 = grads[2][2]
    eps12 = macro[2] + 0.5 * (grads[0][1] + grads[1][0])
    eps13 = 0.5 * (grads[0][2] + grads[2][0])
    eps23 = 0.5 * (grads[1][2] + grads[2][1])
    volume = lame_field * (eps11 + eps22 + eps33)
    twice = 2.0 * shear_field
    return (
        volume + twice * eps11,
        volume + twice * eps22,
        volume + twice * eps33,
        twice * eps12,
        twice * eps13,
        twice * eps23,
    )


def rotate_in(strain, cosine, sine):
    first, second, shear = (strain[0], strain[1], strain[2])
    return jnp.stack(
        [
            cosine * cosine * first + sine * sine * second + 2.0 * cosine * sine * shear,
            sine * sine * first + cosine * cosine * second - 2.0 * cosine * sine * shear,
            -cosine * sine * first
            + cosine * sine * second
            + (cosine * cosine - sine * sine) * shear,
        ]
    )


def rotate_out(stress, cosine, sine):
    first, second, shear = (stress[0], stress[1], stress[2])
    return jnp.stack(
        [
            cosine * cosine * first + sine * sine * second - 2.0 * cosine * sine * shear,
            sine * sine * first + cosine * cosine * second + 2.0 * cosine * sine * shear,
            cosine * sine * first
            - cosine * sine * second
            + (cosine * cosine - sine * sine) * shear,
        ]
    )


def back_diff(field, axis):
    if axis == 0:
        return field[1:] - field[:-1]
    return (field - jnp.roll(field, 1, axis))[1:]


def relax_slab(displace, lame_field, shear_field, macro):
    front = displace[:, :-1]
    grads = [
        [
            displace[i, 1:] - front[i],
            jnp.roll(front[i], -1, 1) - front[i],
            jnp.roll(front[i], -1, 2) - front[i],
        ]
        for i in range(3)
    ]
    s11, s22, s33, s12, s13, s23 = material_stress(grads, lame_field, shear_field, macro)
    first = back_diff(s11, 0) + back_diff(s12, 1) + back_diff(s13, 2)
    second = back_diff(s12, 0) + back_diff(s22, 1) + back_diff(s23, 2)
    third = back_diff(s13, 0) + back_diff(s23, 1) + back_diff(s33, 2)
    shifted = displace[:, 1:-1] + relax_rate * jnp.stack([first, second, third])
    return (shifted, (s11, s22, s12))


def moduli_planes(phase_planes, class_hot):
    fiber_share = phase_planes[0].astype(jnp.float32)[..., None] * class_hot[0]
    for class_number in range(1, NCLASS):
        fiber_share = (
            fiber_share
            + phase_planes[class_number].astype(jnp.float32)[..., None] * class_hot[class_number]
        )
    lame_field = matrix_lame + (fiber_lame - matrix_lame) * fiber_share
    shear_field = matrix_shear + (fiber_shear - matrix_shear) * fiber_share
    return (lame_field, shear_field)


def slot_choice(target, tile_count, capacity, slots):
    highest = lax.Precision.HIGHEST
    row_count = target.shape[0]
    tile_hot = (target[:, None] == jnp.arange(tile_count, dtype=jnp.int32)[None, :]).astype(
        jnp.float32
    )
    row_ids = jnp.arange(row_count, dtype=jnp.int32)
    earlier_mask = (row_ids[:, None] > row_ids[None, :]).astype(jnp.float32)
    earlier = jnp.dot(earlier_mask, tile_hot, precision=highest)
    row_rank = jnp.sum(earlier * tile_hot, axis=1).astype(jnp.int32)
    slot_index = target * capacity + row_rank
    return (slot_index[:, None] == jnp.arange(slots, dtype=jnp.int32)[None, :]).astype(
        jnp.float32
    )


def tile_terms(choose, returned, cosine, sine, heights, elements, per_group):
    highest = lax.Precision.HIGHEST
    point_stress = jnp.dot(choose, returned, precision=highest)
    point_stress = point_stress.T.reshape(3, elements, per_group)
    global_stress = rotate_out(point_stress, cosine, sine)
    weight = 1.0 / TP
    forces = jnp.sum(global_stress, axis=2) * weight
    moments = jnp.sum(global_stress * heights[None, None, :], axis=2) * weight
    return jnp.concatenate([forces, moments], 0)


def node_forces(bmat, terms, connect, node_count):
    highest = lax.Precision.HIGHEST
    corner_force = jnp.einsum("akme,me->ake", bmat, terms, precision=highest)
    node_hot = (
        connect[:, :, None] == jnp.arange(node_count + GHOST, dtype=jnp.int32)[None, None, :]
    ).astype(jnp.float32)
    return jnp.einsum("ake,aen->kn", corner_force, node_hot, precision=highest)


def shift_rows(field, shift, axis):
    if axis == 1:
        size = field.shape[1]
        cut = (size - shift) % size
        return jnp.concatenate([field[:, cut:], field[:, :cut]], 1)
    return pltpu.roll(field, shift % field.shape[axis], axis)


def kernel_sweep(cells, lame_field, shear_field, macro):
    front = [part[:-1] for part in cells]
    grads = [
        [
            cells[i][1:] - front[i],
            shift_rows(front[i], -1, 1) - front[i],
            shift_rows(front[i], -1, 2) - front[i],
        ]
        for i in range(3)
    ]
    s11, s22, s33, s12, s13, s23 = material_stress(grads, lame_field, shear_field, macro)

    def diff(field, axis):
        if axis == 0:
            return field[1:] - field[:-1]
        return (field - shift_rows(field, 1, axis))[1:]

    first = diff(s11, 0) + diff(s12, 1) + diff(s13, 2)
    second = diff(s12, 0) + diff(s22, 1) + diff(s23, 2)
    third = diff(s13, 0) + diff(s23, 1) + diff(s33, 2)
    moved = [
        cells[i][1:-1] + relax_rate * rate_term
        for i, rate_term in enumerate((first, second, third))
    ]
    return (moved, (s11, s22, s12))


def relax_kernel(low_ref, state_ref, high_ref, lame_ref, shear_ref, macro_ref, out_ref, mean_ref):
    rows = state_ref.shape[2]
    depth = ITERS

    def halo_planes(ref, component):
        return [
            ref[pl.ds((component * depth + p) * rows, rows)][None] for p in range(depth)
        ]

    cells = [
        jnp.concatenate(
            halo_planes(low_ref, i) + [state_ref[i]] + halo_planes(high_ref, i), 0
        )
        for i in range(3)
    ]
    lame_all = lame_ref[...]
    shear_all = shear_ref[...]
    macro = [macro_ref[k : k + 1, :].reshape(1, 1, 1, -1) for k in range(3)]
    stress = None
    for round_number in range(ITERS):
        count = cells[0].shape[0]
        cells, stress = kernel_sweep(
            cells,
            lame_all[round_number : round_number + count - 1],
            shear_all[round_number : round_number + count - 1],
            macro,
        )
    for i in range(3):
        out_ref[i] = cells[i]
    for k in range(3):
        total = jnp.sum(stress[k][1:], axis=(0, 1))
        mean_ref[k : k + 1, :] = jnp.sum(total, axis=0, keepdims=True) / float(RES**3)


def relax_slab_kernel(low, state, high, lame_field, shear_field, macro):
    out_shape = (
        jax.ShapeDtypeStruct(state.shape, jnp.float32),
        jax.ShapeDtypeStruct((3, state.shape[-1]), jnp.float32),
    )
    return pl.pallas_call(
        relax_kernel,
        out_shape=out_shape,
        in_specs=[pl.BlockSpec(memory_space=pltpu.VMEM)] * 6,
        out_specs=(pl.BlockSpec(memory_space=pltpu.VMEM), pl.BlockSpec(memory_space=pltpu.VMEM)),
        compiler_params=pltpu.CompilerParams(vmem_limit_bytes=60 * 1024 * 1024),
    )(low, state, high, lame_field, shear_field, macro)


def halo_pack(cells, phase_planes):
    lanes = cells.shape[-1]
    rows = cells.shape[-2]
    flat_cells = cells.reshape(-1, rows, lanes)
    flat_phase = phase_planes.astype(jnp.float32).reshape(-1, rows, lanes)
    return jnp.concatenate([flat_cells, flat_phase], 0)


def halo_unpack(moved, phase_planes):
    count = moved.shape[0] - phase_planes.size // (moved.shape[1] * moved.shape[2])
    return moved[count:].reshape(phase_planes.shape).astype(jnp.int32)


def shards(
    gen_strain, ply_class, route, phase, rve_state, connect, bmat, velocity, force_ext, mass
):
    highest = lax.Precision.HIGHEST
    thick_index = lax.axis_index("thick")
    per_group = route.shape[2]
    elements = gen_strain.shape[1]
    tile_count = lax.axis_size("tile")
    slab_count = lax.axis_size("rve")
    slots = rve_state.shape[4]
    capacity = slots // tile_count
    row_count = elements * per_group
    depth = ITERS
    up = [(i, (i + 1) % slab_count) for i in range(slab_count)]
    down = [((i + 1) % slab_count, i) for i in range(slab_count)]
    planes = rve_state.shape[1]
    low_side = phase[:, planes - depth :]
    high_side = phase[:, :depth]
    pack_up = halo_pack(rve_state[:, planes - depth :], low_side)
    pack_down = halo_pack(rve_state[:, :depth], high_side)
    route_rows = route.reshape(elements, per_group).T
    int_rows = jnp.concatenate([route_rows, connect], 0)
    flat_bmat = bmat.reshape(-1, elements)
    layer = thick_index * per_group + jnp.arange(per_group, dtype=jnp.int32)
    heights = -1.0 + (2.0 * layer.astype(jnp.float32) + 1.0) / TP
    classes = lax.dynamic_slice_in_dim(ply_class, thick_index * per_group, per_group)
    angle = classes.astype(jnp.float32) * (math.pi / NCLASS)
    cosine = jnp.cos(angle)[None, :]
    sine = jnp.sin(angle)[None, :]
    membrane = gen_strain[:3][:, :, None]
    bending = gen_strain[3:][:, :, None]
    point_strain = membrane + heights[None, None, :] * bending
    rotated = rotate_in(point_strain, cosine, sine)
    row_class = jnp.broadcast_to(classes[None, :], (elements, per_group)).reshape(row_count)
    payload = jnp.concatenate(
        [rotated.reshape(3, row_count), row_class.astype(jnp.float32)[None, :]], 0
    ).T
    choose = slot_choice(route.reshape(row_count), tile_count, capacity, slots)
    send = jnp.dot(choose.T, payload, precision=highest)
    send, pack_up, pack_down = lax.optimization_barrier((send, pack_up, pack_down))
    below = lax.ppermute(pack_up, "rve", up)
    above = lax.ppermute(pack_down, "rve", down)
    phase_below = halo_unpack(below, low_side)
    phase_above = halo_unpack(above, high_side)
    received = lax.all_to_all(
        send.reshape(tile_count, capacity, 4), "tile", split_axis=0, concat_axis=0, tiled=True
    ).reshape(slots, 4)
    macro = received[:, :3].T
    slot_class = received[:, 3].astype(jnp.int32)
    class_hot = (slot_class[None, :] == jnp.arange(NCLASS, dtype=jnp.int32)[:, None]).astype(
        jnp.float32
    )
    wide_phase = jnp.concatenate([phase_below, phase, phase_above], 1)
    lame_field, shear_field = moduli_planes(wide_phase, class_hot)
    displace, average = relax_slab_kernel(below, rve_state, above, lame_field, shear_field, macro)
    ghost_rows = jnp.concatenate([flat_bmat, int_rows.astype(jnp.float32)], 0)
    prev_pack = from_behind(ghost_rows + 0.0 * average[0, 0], "tile", 1)
    own_chunks = average.T.reshape(tile_count, capacity, 3)
    both_chunks = jnp.concatenate([own_chunks, jnp.roll(own_chunks, 1, axis=0)], 1)
    returned = lax.all_to_all(both_chunks, "tile", split_axis=0, concat_axis=0, tiled=True)
    own_returned = returned[:, :capacity].reshape(slots, 3)
    prev_returned = returned[:, capacity:].reshape(slots, 3)
    own_terms = tile_terms(choose, own_returned, cosine, sine, heights, elements, per_group)
    prev_bmat = prev_pack[: flat_bmat.shape[0]].reshape(bmat.shape)
    prev_ints = prev_pack[flat_bmat.shape[0] :].astype(jnp.int32)
    prev_route = prev_ints[:per_group].T.reshape(row_count)
    prev_connect = prev_ints[per_group:]
    prev_choose = slot_choice(prev_route, tile_count, capacity, slots)
    prev_terms = tile_terms(prev_choose, prev_returned, cosine, sine, heights, elements, per_group)
    node_count = velocity.shape[1]
    own_nodes = node_forces(bmat, own_terms, connect, node_count)[:, :node_count]
    ghost_nodes = node_forces(prev_bmat, prev_terms, prev_connect, node_count)[:, node_count:]
    partial_internal = own_nodes.at[:, :GHOST].add(ghost_nodes)
    totals = lax.psum(lax.psum(jnp.concatenate([own_terms, partial_internal], 0), "rve"), "thick")
    resultants = totals[:6]
    internal = totals[6:]
    new_velocity = velocity + time_step * (force_ext - internal) / mass[None, :]
    return (new_velocity, resultants, displace)


def solution(mesh):
    placed = (
        P(None, "tile"),
        P(),
        P("thick", "tile", None, None),
        P(None, "rve", None, None),
        P(None, "rve", None, None, ("tile", "thick")),
        P(None, "tile"),
        P(None, None, None, "tile"),
        P(None, "tile"),
        P(None, "tile"),
        P("tile"),
    )
    return jax.shard_map(
        shards,
        mesh=mesh,
        in_specs=placed,
        out_specs=(P(None, "tile"), P(None, "tile"), P(None, "rve", None, None, ("tile", "thick"))),
        check_vma=False,
    )
```

```python
import math

import jax
import jax.numpy as jnp
from jax import lax
from jax.experimental import pallas as pl
from jax.experimental.pallas import tpu as pltpu
from jax.sharding import PartitionSpec as P

TP = 8
NCLASS = 4
RES = 16
ITERS = 2
GHOST = 8


matrix_lame = 1.2
matrix_shear = 0.8
fiber_lame = 8.0
fiber_shear = 5.0
relax_rate = 1.0 / 288.0
time_step = 0.25


def with_halo(cells, sides, width):
    for axis, dim in sides:
        count = lax.axis_size(axis)
        head = lax.slice_in_dim(cells, 0, width, axis=dim)
        tail = lax.slice_in_dim(cells, cells.shape[dim] - width, cells.shape[dim], axis=dim)
        cells = jnp.concatenate(
            [
                lax.ppermute(tail, axis, [(i, (i + 1) % count) for i in range(count)]),
                cells,
                lax.ppermute(head, axis, [((i + 1) % count, i) for i in range(count)]),
            ],
            axis=dim,
        )
    return cells


def from_behind(value, axis, steps):
    count = lax.axis_size(axis)
    pairs = [(source, (source + steps) % count) for source in range(count)]
    return lax.ppermute(value, axis, pairs)


def material_stress(grads, lame_field, shear_field, macro):
    eps11 = macro[0] + grads[0][0]
    eps22 = macro[1] + grads[1][1]
    eps33 = grads[2][2]
    eps12 = macro[2] + 0.5 * (grads[0][1] + grads[1][0])
    eps13 = 0.5 * (grads[0][2] + grads[2][0])
    eps23 = 0.5 * (grads[1][2] + grads[2][1])
    volume = lame_field * (eps11 + eps22 + eps33)
    twice = 2.0 * shear_field
    return (
        volume + twice * eps11,
        volume + twice * eps22,
        volume + twice * eps33,
        twice * eps12,
        twice * eps13,
        twice * eps23,
    )


def rotate_in(strain, cosine, sine):
    first, second, shear = (strain[0], strain[1], strain[2])
    return jnp.stack(
        [
            cosine * cosine * first + sine * sine * second + 2.0 * cosine * sine * shear,
            sine * sine * first + cosine * cosine * second - 2.0 * cosine * sine * shear,
            -cosine * sine * first
            + cosine * sine * second
            + (cosine * cosine - sine * sine) * shear,
        ]
    )


def rotate_out(stress, cosine, sine):
    first, second, shear = (stress[0], stress[1], stress[2])
    return jnp.stack(
        [
            cosine * cosine * first + sine * sine * second - 2.0 * cosine * sine * shear,
            sine * sine * first + cosine * cosine * second + 2.0 * cosine * sine * shear,
            cosine * sine * first
            - cosine * sine * second
            + (cosine * cosine - sine * sine) * shear,
        ]
    )


def back_diff(field, axis):
    if axis == 0:
        return field[1:] - field[:-1]
    return (field - jnp.roll(field, 1, axis))[1:]


def relax_slab(displace, lame_field, shear_field, macro):
    front = displace[:, :-1]
    grads = [
        [
            displace[i, 1:] - front[i],
            jnp.roll(front[i], -1, 1) - front[i],
            jnp.roll(front[i], -1, 2) - front[i],
        ]
        for i in range(3)
    ]
    s11, s22, s33, s12, s13, s23 = material_stress(grads, lame_field, shear_field, macro)
    first = back_diff(s11, 0) + back_diff(s12, 1) + back_diff(s13, 2)
    second = back_diff(s12, 0) + back_diff(s22, 1) + back_diff(s23, 2)
    third = back_diff(s13, 0) + back_diff(s23, 1) + back_diff(s33, 2)
    shifted = displace[:, 1:-1] + relax_rate * jnp.stack([first, second, third])
    return (shifted, (s11, s22, s12))


def moduli_planes(phase_planes, class_hot):
    fiber_share = phase_planes[0].astype(jnp.float32)[..., None] * class_hot[0]
    for class_number in range(1, NCLASS):
        fiber_share = (
            fiber_share
            + phase_planes[class_number].astype(jnp.float32)[..., None] * class_hot[class_number]
        )
    lame_field = matrix_lame + (fiber_lame - matrix_lame) * fiber_share
    shear_field = matrix_shear + (fiber_shear - matrix_shear) * fiber_share
    return (lame_field, shear_field)


def slot_choice(target, tile_count, capacity, slots):
    highest = lax.Precision.HIGHEST
    row_count = target.shape[0]
    tile_hot = (target[:, None] == jnp.arange(tile_count, dtype=jnp.int32)[None, :]).astype(
        jnp.float32
    )
    row_ids = jnp.arange(row_count, dtype=jnp.int32)
    earlier_mask = (row_ids[:, None] > row_ids[None, :]).astype(jnp.float32)
    earlier = jnp.dot(earlier_mask, tile_hot, precision=highest)
    row_rank = jnp.sum(earlier * tile_hot, axis=1).astype(jnp.int32)
    slot_index = target * capacity + row_rank
    return (slot_index[:, None] == jnp.arange(slots, dtype=jnp.int32)[None, :]).astype(
        jnp.float32
    )


def tile_terms(choose, returned, cosine, sine, heights, elements, per_group):
    highest = lax.Precision.HIGHEST
    point_stress = jnp.dot(choose, returned, precision=highest)
    point_stress = point_stress.T.reshape(3, elements, per_group)
    global_stress = rotate_out(point_stress, cosine, sine)
    weight = 1.0 / TP
    forces = jnp.sum(global_stress, axis=2) * weight
    moments = jnp.sum(global_stress * heights[None, None, :], axis=2) * weight
    return jnp.concatenate([forces, moments], 0)


def node_forces(bmat, terms, connect, node_count):
    highest = lax.Precision.HIGHEST
    corner_force = jnp.einsum("akme,me->ake", bmat, terms, precision=highest)
    node_hot = (
        connect[:, :, None] == jnp.arange(node_count + GHOST, dtype=jnp.int32)[None, None, :]
    ).astype(jnp.float32)
    return jnp.einsum("ake,aen->kn", corner_force, node_hot, precision=highest)


def shift_rows(field, shift, axis):
    if axis == 1:
        size = field.shape[1]
        cut = (size - shift) % size
        return jnp.concatenate([field[:, cut:], field[:, :cut]], 1)
    return pltpu.roll(field, shift % field.shape[axis], axis)


def kernel_sweep(cells, lame_field, shear_field, macro):
    front = [part[:-1] for part in cells]
    grads = [
        [
            cells[i][1:] - front[i],
            shift_rows(front[i], -1, 1) - front[i],
            shift_rows(front[i], -1, 2) - front[i],
        ]
        for i in range(3)
    ]
    s11, s22, s33, s12, s13, s23 = material_stress(grads, lame_field, shear_field, macro)

    def diff(field, axis):
        if axis == 0:
            return field[1:] - field[:-1]
        return (field - shift_rows(field, 1, axis))[1:]

    first = diff(s11, 0) + diff(s12, 1) + diff(s13, 2)
    second = diff(s12, 0) + diff(s22, 1) + diff(s23, 2)
    third = diff(s13, 0) + diff(s23, 1) + diff(s33, 2)
    moved = [
        cells[i][1:-1] + relax_rate * rate_term
        for i, rate_term in enumerate((first, second, third))
    ]
    return (moved, (s11, s22, s12))


def relax_kernel(low_ref, state_ref, high_ref, lame_ref, shear_ref, macro_ref, out_ref, mean_ref):
    rows = state_ref.shape[2]
    depth = ITERS

    def halo_planes(ref, component):
        return [
            ref[pl.ds((component * depth + p) * rows, rows)][None] for p in range(depth)
        ]

    cells = [
        jnp.concatenate(
            halo_planes(low_ref, i) + [state_ref[i]] + halo_planes(high_ref, i), 0
        )
        for i in range(3)
    ]
    lame_all = lame_ref[...]
    shear_all = shear_ref[...]
    macro = [macro_ref[k : k + 1, :].reshape(1, 1, 1, -1) for k in range(3)]
    stress = None
    for round_number in range(ITERS):
        count = cells[0].shape[0]
        cells, stress = kernel_sweep(
            cells,
            lame_all[round_number : round_number + count - 1],
            shear_all[round_number : round_number + count - 1],
            macro,
        )
    for i in range(3):
        out_ref[i] = cells[i]
    for k in range(3):
        total = jnp.sum(stress[k][1:], axis=(0, 1))
        mean_row = jnp.sum(total, axis=0, keepdims=True) / float(RES**3)
        mean_ref[k : k + 1, :] = mean_row
        mean_ref[3 + k : 4 + k, :] = pltpu.roll(mean_row, 2, 1)


def relax_slab_kernel(low, state, high, lame_field, shear_field, macro):
    out_shape = (
        jax.ShapeDtypeStruct(state.shape, jnp.float32),
        jax.ShapeDtypeStruct((6, state.shape[-1]), jnp.float32),
    )
    return pl.pallas_call(
        relax_kernel,
        out_shape=out_shape,
        in_specs=[pl.BlockSpec(memory_space=pltpu.VMEM)] * 6,
        out_specs=(pl.BlockSpec(memory_space=pltpu.VMEM), pl.BlockSpec(memory_space=pltpu.VMEM)),
        compiler_params=pltpu.CompilerParams(vmem_limit_bytes=60 * 1024 * 1024),
    )(low, state, high, lame_field, shear_field, macro)


def halo_pack(cells, phase_planes):
    lanes = cells.shape[-1]
    rows = cells.shape[-2]
    flat_cells = cells.reshape(-1, rows, lanes)
    flat_phase = phase_planes.astype(jnp.float32).reshape(-1, rows, lanes)
    return jnp.concatenate([flat_cells, flat_phase], 0)


def halo_unpack(moved, phase_planes):
    count = moved.shape[0] - phase_planes.size // (moved.shape[1] * moved.shape[2])
    return moved[count:].reshape(phase_planes.shape).astype(jnp.int32)


def shards(
    gen_strain, ply_class, route, phase, rve_state, connect, bmat, velocity, force_ext, mass
):
    highest = lax.Precision.HIGHEST
    thick_index = lax.axis_index("thick")
    per_group = route.shape[2]
    elements = gen_strain.shape[1]
    tile_count = lax.axis_size("tile")
    slab_count = lax.axis_size("rve")
    slots = rve_state.shape[4]
    capacity = slots // tile_count
    row_count = elements * per_group
    depth = ITERS
    up = [(i, (i + 1) % slab_count) for i in range(slab_count)]
    down = [((i + 1) % slab_count, i) for i in range(slab_count)]
    planes = rve_state.shape[1]
    low_side = phase[:, planes - depth :]
    high_side = phase[:, :depth]
    pack_up = halo_pack(rve_state[:, planes - depth :], low_side)
    pack_down = halo_pack(rve_state[:, :depth], high_side)
    route_rows = route.reshape(elements, per_group).T
    int_rows = jnp.concatenate([route_rows, connect], 0)
    flat_bmat = bmat.reshape(-1, elements)
    layer = thick_index * per_group + jnp.arange(per_group, dtype=jnp.int32)
    heights = -1.0 + (2.0 * layer.astype(jnp.float32) + 1.0) / TP
    classes = lax.dynamic_slice_in_dim(ply_class, thick_index * per_group, per_group)
    angle = classes.astype(jnp.float32) * (math.pi / NCLASS)
    cosine = jnp.cos(angle)[None, :]
    sine = jnp.sin(angle)[None, :]
    membrane = gen_strain[:3][:, :, None]
    bending = gen_strain[3:][:, :, None]
    point_strain = membrane + heights[None, None, :] * bending
    rotated = rotate_in(point_strain, cosine, sine)
    row_class = jnp.broadcast_to(classes[None, :], (elements, per_group)).reshape(row_count)
    payload = jnp.concatenate(
        [rotated.reshape(3, row_count), row_class.astype(jnp.float32)[None, :]], 0
    ).T
    choose = slot_choice(route.reshape(row_count), tile_count, capacity, slots)
    send = jnp.dot(choose.T, payload, precision=highest)
    send, pack_up, pack_down = lax.optimization_barrier((send, pack_up, pack_down))
    below = lax.ppermute(pack_up, "rve", up)
    above = lax.ppermute(pack_down, "rve", down)
    phase_below = halo_unpack(below, low_side)
    phase_above = halo_unpack(above, high_side)
    received = lax.all_to_all(
        send.reshape(tile_count, capacity, 4), "tile", split_axis=0, concat_axis=0, tiled=True
    ).reshape(slots, 4)
    macro = received[:, :3].T
    slot_class = received[:, 3].astype(jnp.int32)
    class_hot = (slot_class[None, :] == jnp.arange(NCLASS, dtype=jnp.int32)[:, None]).astype(
        jnp.float32
    )
    wide_phase = jnp.concatenate([phase_below, phase, phase_above], 1)
    lame_field, shear_field = moduli_planes(wide_phase, class_hot)
    displace, average = relax_slab_kernel(below, rve_state, above, lame_field, shear_field, macro)
    ghost_rows = jnp.concatenate([flat_bmat, int_rows.astype(jnp.float32)], 0)
    ghost_rows, average = lax.optimization_barrier((ghost_rows, average))
    prev_pack = from_behind(ghost_rows, "tile", 1)
    both_chunks = (
        average.reshape(2, 3, tile_count, capacity)
        .transpose(2, 0, 3, 1)
        .reshape(tile_count, 2 * capacity, 3)
    )
    returned = lax.all_to_all(both_chunks, "tile", split_axis=0, concat_axis=0, tiled=True)
    own_returned = returned[:, :capacity].reshape(slots, 3)
    prev_returned = returned[:, capacity:].reshape(slots, 3)
    own_terms = tile_terms(choose, own_returned, cosine, sine, heights, elements, per_group)
    prev_bmat = prev_pack[: flat_bmat.shape[0]].reshape(bmat.shape)
    prev_ints = prev_pack[flat_bmat.shape[0] :].astype(jnp.int32)
    prev_route = prev_ints[:per_group].T.reshape(row_count)
    prev_connect = prev_ints[per_group:]
    prev_choose = slot_choice(prev_route, tile_count, capacity, slots)
    prev_terms = tile_terms(prev_choose, prev_returned, cosine, sine, heights, elements, per_group)
    node_count = velocity.shape[1]
    own_nodes = node_forces(bmat, own_terms, connect, node_count)[:, :node_count]
    ghost_nodes = node_forces(prev_bmat, prev_terms, prev_connect, node_count)[:, node_count:]
    partial_internal = own_nodes.at[:, :GHOST].add(ghost_nodes)
    totals = lax.psum(lax.psum(jnp.concatenate([own_terms, partial_internal], 0), "rve"), "thick")
    resultants = totals[:6]
    internal = totals[6:]
    new_velocity = velocity + time_step * (force_ext - internal) / mass[None, :]
    return (new_velocity, resultants, displace)


def solution(mesh):
    placed = (
        P(None, "tile"),
        P(),
        P("thick", "tile", None, None),
        P(None, "rve", None, None),
        P(None, "rve", None, None, ("tile", "thick")),
        P(None, "tile"),
        P(None, None, None, "tile"),
        P(None, "tile"),
        P(None, "tile"),
        P("tile"),
    )
    return jax.shard_map(
        shards,
        mesh=mesh,
        in_specs=placed,
        out_specs=(P(None, "tile"), P(None, "tile"), P(None, "rve", None, None, ("tile", "thick"))),
        check_vma=False,
    )
```

```python
import math

import jax
import jax.numpy as jnp
from jax import lax
from jax.experimental import pallas as pl
from jax.experimental.pallas import tpu as pltpu
from jax.sharding import PartitionSpec as P

TP = 8
NCLASS = 4
RES = 16
ITERS = 2
GHOST = 8


matrix_lame = 1.2
matrix_shear = 0.8
fiber_lame = 8.0
fiber_shear = 5.0
relax_rate = 1.0 / 288.0
time_step = 0.25


def with_halo(cells, sides, width):
    for axis, dim in sides:
        count = lax.axis_size(axis)
        head = lax.slice_in_dim(cells, 0, width, axis=dim)
        tail = lax.slice_in_dim(cells, cells.shape[dim] - width, cells.shape[dim], axis=dim)
        cells = jnp.concatenate(
            [
                lax.ppermute(tail, axis, [(i, (i + 1) % count) for i in range(count)]),
                cells,
                lax.ppermute(head, axis, [((i + 1) % count, i) for i in range(count)]),
            ],
            axis=dim,
        )
    return cells


def from_behind(value, axis, steps):
    count = lax.axis_size(axis)
    pairs = [(source, (source + steps) % count) for source in range(count)]
    return lax.ppermute(value, axis, pairs)


def material_stress(grads, lame_field, shear_field, macro):
    eps11 = macro[0] + grads[0][0]
    eps22 = macro[1] + grads[1][1]
    eps33 = grads[2][2]
    eps12 = macro[2] + 0.5 * (grads[0][1] + grads[1][0])
    eps13 = 0.5 * (grads[0][2] + grads[2][0])
    eps23 = 0.5 * (grads[1][2] + grads[2][1])
    volume = lame_field * (eps11 + eps22 + eps33)
    twice = 2.0 * shear_field
    return (
        volume + twice * eps11,
        volume + twice * eps22,
        volume + twice * eps33,
        twice * eps12,
        twice * eps13,
        twice * eps23,
    )


def rotate_in(strain, cosine, sine):
    first, second, shear = (strain[0], strain[1], strain[2])
    return jnp.stack(
        [
            cosine * cosine * first + sine * sine * second + 2.0 * cosine * sine * shear,
            sine * sine * first + cosine * cosine * second - 2.0 * cosine * sine * shear,
            -cosine * sine * first
            + cosine * sine * second
            + (cosine * cosine - sine * sine) * shear,
        ]
    )


def rotate_out(stress, cosine, sine):
    first, second, shear = (stress[0], stress[1], stress[2])
    return jnp.stack(
        [
            cosine * cosine * first + sine * sine * second - 2.0 * cosine * sine * shear,
            sine * sine * first + cosine * cosine * second + 2.0 * cosine * sine * shear,
            cosine * sine * first
            - cosine * sine * second
            + (cosine * cosine - sine * sine) * shear,
        ]
    )


def back_diff(field, axis):
    if axis == 0:
        return field[1:] - field[:-1]
    return (field - jnp.roll(field, 1, axis))[1:]


def relax_slab(displace, lame_field, shear_field, macro):
    front = displace[:, :-1]
    grads = [
        [
            displace[i, 1:] - front[i],
            jnp.roll(front[i], -1, 1) - front[i],
            jnp.roll(front[i], -1, 2) - front[i],
        ]
        for i in range(3)
    ]
    s11, s22, s33, s12, s13, s23 = material_stress(grads, lame_field, shear_field, macro)
    first = back_diff(s11, 0) + back_diff(s12, 1) + back_diff(s13, 2)
    second = back_diff(s12, 0) + back_diff(s22, 1) + back_diff(s23, 2)
    third = back_diff(s13, 0) + back_diff(s23, 1) + back_diff(s33, 2)
    shifted = displace[:, 1:-1] + relax_rate * jnp.stack([first, second, third])
    return (shifted, (s11, s22, s12))


def share_planes(phase_planes, class_hot):
    fiber_share = phase_planes[0].astype(jnp.float32)[..., None] * class_hot[0]
    for class_number in range(1, NCLASS):
        fiber_share = (
            fiber_share
            + phase_planes[class_number].astype(jnp.float32)[..., None] * class_hot[class_number]
        )
    return fiber_share


def moduli_planes(phase_planes, class_hot):
    fiber_share = phase_planes[0].astype(jnp.float32)[..., None] * class_hot[0]
    for class_number in range(1, NCLASS):
        fiber_share = (
            fiber_share
            + phase_planes[class_number].astype(jnp.float32)[..., None] * class_hot[class_number]
        )
    lame_field = matrix_lame + (fiber_lame - matrix_lame) * fiber_share
    shear_field = matrix_shear + (fiber_shear - matrix_shear) * fiber_share
    return (lame_field, shear_field)


def slot_choice(target, tile_count, capacity, slots):
    highest = lax.Precision.HIGHEST
    row_count = target.shape[0]
    tile_hot = (target[:, None] == jnp.arange(tile_count, dtype=jnp.int32)[None, :]).astype(
        jnp.float32
    )
    row_ids = jnp.arange(row_count, dtype=jnp.int32)
    earlier_mask = (row_ids[:, None] > row_ids[None, :]).astype(jnp.float32)
    earlier = jnp.dot(earlier_mask, tile_hot, precision=highest)
    row_rank = jnp.sum(earlier * tile_hot, axis=1).astype(jnp.int32)
    slot_index = target * capacity + row_rank
    return (slot_index[:, None] == jnp.arange(slots, dtype=jnp.int32)[None, :]).astype(
        jnp.float32
    )


def tile_terms(choose, returned, cosine, sine, heights, elements, per_group):
    highest = lax.Precision.HIGHEST
    point_stress = jnp.dot(choose, returned, precision=highest)
    point_stress = point_stress.T.reshape(3, elements, per_group)
    global_stress = rotate_out(point_stress, cosine, sine)
    weight = 1.0 / TP
    forces = jnp.sum(global_stress, axis=2) * weight
    moments = jnp.sum(global_stress * heights[None, None, :], axis=2) * weight
    return jnp.concatenate([forces, moments], 0)


def node_forces(bmat, terms, connect, node_count):
    highest = lax.Precision.HIGHEST
    corner_force = jnp.einsum("akme,me->ake", bmat, terms, precision=highest)
    node_hot = (
        connect[:, :, None] == jnp.arange(node_count + GHOST, dtype=jnp.int32)[None, None, :]
    ).astype(jnp.float32)
    return jnp.einsum("ake,aen->kn", corner_force, node_hot, precision=highest)


def shift_rows(field, shift, axis):
    if axis == 1:
        size = field.shape[1]
        cut = (size - shift) % size
        return jnp.concatenate([field[:, cut:], field[:, :cut]], 1)
    return pltpu.roll(field, shift % field.shape[axis], axis)


def kernel_sweep(cells, lame_field, shear_field, macro):
    front = [part[:-1] for part in cells]
    grads = [
        [
            cells[i][1:] - front[i],
            shift_rows(front[i], -1, 1) - front[i],
            shift_rows(front[i], -1, 2) - front[i],
        ]
        for i in range(3)
    ]
    s11, s22, s33, s12, s13, s23 = material_stress(grads, lame_field, shear_field, macro)

    def diff(field, axis):
        if axis == 0:
            return field[1:] - field[:-1]
        return (field - shift_rows(field, 1, axis))[1:]

    first = diff(s11, 0) + diff(s12, 1) + diff(s13, 2)
    second = diff(s12, 0) + diff(s22, 1) + diff(s23, 2)
    third = diff(s13, 0) + diff(s23, 1) + diff(s33, 2)
    moved = [
        cells[i][1:-1] + relax_rate * rate_term
        for i, rate_term in enumerate((first, second, third))
    ]
    return (moved, (s11, s22, s12))


def relax_kernel(low_ref, state_ref, high_ref, share_ref, macro_ref, out_ref, mean_ref):
    rows = state_ref.shape[2]
    depth = ITERS

    def halo_planes(ref, component):
        return [
            ref[pl.ds((component * depth + p) * rows, rows)][None] for p in range(depth)
        ]

    cells = [
        jnp.concatenate(
            halo_planes(low_ref, i) + [state_ref[i]] + halo_planes(high_ref, i), 0
        )
        for i in range(3)
    ]
    fiber_share = share_ref[...]
    lame_all = matrix_lame + (fiber_lame - matrix_lame) * fiber_share
    shear_all = matrix_shear + (fiber_shear - matrix_shear) * fiber_share
    macro = [macro_ref[k : k + 1, :].reshape(1, 1, 1, -1) for k in range(3)]
    stress = None
    for round_number in range(ITERS):
        count = cells[0].shape[0]
        cells, stress = kernel_sweep(
            cells,
            lame_all[round_number : round_number + count - 1],
            shear_all[round_number : round_number + count - 1],
            macro,
        )
    for i in range(3):
        out_ref[i] = cells[i]
    for k in range(3):
        total = jnp.sum(stress[k][1:], axis=(0, 1))
        mean_row = jnp.sum(total, axis=0, keepdims=True) / float(RES**3)
        mean_ref[k : k + 1, :] = mean_row
        mean_ref[3 + k : 4 + k, :] = pltpu.roll(mean_row, 2, 1)


def relax_slab_kernel(low, state, high, fiber_share, macro):
    out_shape = (
        jax.ShapeDtypeStruct(state.shape, jnp.float32),
        jax.ShapeDtypeStruct((6, state.shape[-1]), jnp.float32),
    )
    return pl.pallas_call(
        relax_kernel,
        out_shape=out_shape,
        in_specs=[pl.BlockSpec(memory_space=pltpu.VMEM)] * 5,
        out_specs=(pl.BlockSpec(memory_space=pltpu.VMEM), pl.BlockSpec(memory_space=pltpu.VMEM)),
        compiler_params=pltpu.CompilerParams(vmem_limit_bytes=60 * 1024 * 1024),
    )(low, state, high, fiber_share, macro)


def halo_pack(cells, phase_planes):
    lanes = cells.shape[-1]
    rows = cells.shape[-2]
    flat_cells = cells.reshape(-1, rows, lanes)
    flat_phase = phase_planes.astype(jnp.float32).reshape(-1, rows, lanes)
    return jnp.concatenate([flat_cells, flat_phase], 0)


def halo_unpack(moved, phase_planes):
    count = moved.shape[0] - phase_planes.size // (moved.shape[1] * moved.shape[2])
    return moved[count:].reshape(phase_planes.shape).astype(jnp.int32)


def shards(
    gen_strain, ply_class, route, phase, rve_state, connect, bmat, velocity, force_ext, mass
):
    highest = lax.Precision.HIGHEST
    thick_index = lax.axis_index("thick")
    per_group = route.shape[2]
    elements = gen_strain.shape[1]
    tile_count = lax.axis_size("tile")
    slab_count = lax.axis_size("rve")
    slots = rve_state.shape[4]
    capacity = slots // tile_count
    row_count = elements * per_group
    depth = ITERS
    up = [(i, (i + 1) % slab_count) for i in range(slab_count)]
    down = [((i + 1) % slab_count, i) for i in range(slab_count)]
    planes = rve_state.shape[1]
    low_side = phase[:, planes - depth :]
    high_side = phase[:, :depth]
    pack_up = halo_pack(rve_state[:, planes - depth :], low_side)
    pack_down = halo_pack(rve_state[:, :depth], high_side)
    route_rows = route.reshape(elements, per_group).T
    int_rows = jnp.concatenate([route_rows, connect], 0)
    flat_bmat = bmat.reshape(-1, elements)
    layer = thick_index * per_group + jnp.arange(per_group, dtype=jnp.int32)
    heights = -1.0 + (2.0 * layer.astype(jnp.float32) + 1.0) / TP
    classes = lax.dynamic_slice_in_dim(ply_class, thick_index * per_group, per_group)
    angle = classes.astype(jnp.float32) * (math.pi / NCLASS)
    cosine = jnp.cos(angle)[None, :]
    sine = jnp.sin(angle)[None, :]
    membrane = gen_strain[:3][:, :, None]
    bending = gen_strain[3:][:, :, None]
    point_strain = membrane + heights[None, None, :] * bending
    rotated = rotate_in(point_strain, cosine, sine)
    row_class = jnp.broadcast_to(classes[None, :], (elements, per_group)).reshape(row_count)
    payload = jnp.concatenate(
        [rotated.reshape(3, row_count), row_class.astype(jnp.float32)[None, :]], 0
    ).T
    choose = slot_choice(route.reshape(row_count), tile_count, capacity, slots)
    send = jnp.dot(choose.T, payload, precision=highest)
    send, pack_up, pack_down = lax.optimization_barrier((send, pack_up, pack_down))
    below = lax.ppermute(pack_up, "rve", up)
    above = lax.ppermute(pack_down, "rve", down)
    phase_below = halo_unpack(below, low_side)
    phase_above = halo_unpack(above, high_side)
    received = lax.all_to_all(
        send.reshape(tile_count, capacity, 4), "tile", split_axis=0, concat_axis=0, tiled=True
    ).reshape(slots, 4)
    macro = received[:, :3].T
    slot_class = received[:, 3].astype(jnp.int32)
    class_hot = (slot_class[None, :] == jnp.arange(NCLASS, dtype=jnp.int32)[:, None]).astype(
        jnp.float32
    )
    wide_phase = jnp.concatenate([phase_below, phase, phase_above], 1)
    fiber_share = share_planes(wide_phase, class_hot)
    displace, average = relax_slab_kernel(below, rve_state, above, fiber_share, macro)
    ghost_rows = jnp.concatenate([flat_bmat, int_rows.astype(jnp.float32)], 0)
    ghost_rows, average = lax.optimization_barrier((ghost_rows, average))
    prev_pack = from_behind(ghost_rows, "tile", 1)
    both_chunks = (
        average.reshape(2, 3, tile_count, capacity)
        .transpose(2, 0, 3, 1)
        .reshape(tile_count, 2 * capacity, 3)
    )
    returned = lax.all_to_all(both_chunks, "tile", split_axis=0, concat_axis=0, tiled=True)
    own_returned = returned[:, :capacity].reshape(slots, 3)
    prev_returned = returned[:, capacity:].reshape(slots, 3)
    own_terms = tile_terms(choose, own_returned, cosine, sine, heights, elements, per_group)
    prev_bmat = prev_pack[: flat_bmat.shape[0]].reshape(bmat.shape)
    prev_ints = prev_pack[flat_bmat.shape[0] :].astype(jnp.int32)
    prev_route = prev_ints[:per_group].T.reshape(row_count)
    prev_connect = prev_ints[per_group:]
    prev_choose = slot_choice(prev_route, tile_count, capacity, slots)
    prev_terms = tile_terms(prev_choose, prev_returned, cosine, sine, heights, elements, per_group)
    node_count = velocity.shape[1]
    own_nodes = node_forces(bmat, own_terms, connect, node_count)[:, :node_count]
    ghost_nodes = node_forces(prev_bmat, prev_terms, prev_connect, node_count)[:, node_count:]
    partial_internal = own_nodes.at[:, :GHOST].add(ghost_nodes)
    totals = lax.psum(lax.psum(jnp.concatenate([own_terms, partial_internal], 0), "rve"), "thick")
    resultants = totals[:6]
    internal = totals[6:]
    new_velocity = velocity + time_step * (force_ext - internal) / mass[None, :]
    return (new_velocity, resultants, displace)


def solution(mesh):
    placed = (
        P(None, "tile"),
        P(),
        P("thick", "tile", None, None),
        P(None, "rve", None, None),
        P(None, "rve", None, None, ("tile", "thick")),
        P(None, "tile"),
        P(None, None, None, "tile"),
        P(None, "tile"),
        P(None, "tile"),
        P("tile"),
    )
    return jax.shard_map(
        shards,
        mesh=mesh,
        in_specs=placed,
        out_specs=(P(None, "tile"), P(None, "tile"), P(None, "rve", None, None, ("tile", "thick"))),
        check_vma=False,
    )
```

```python
import math

import jax
import jax.numpy as jnp
from jax import lax
from jax.experimental import pallas as pl
from jax.experimental.pallas import tpu as pltpu
from jax.sharding import PartitionSpec as P

TP = 8
NCLASS = 4
RES = 16
ITERS = 2
GHOST = 8


matrix_lame = 1.2
matrix_shear = 0.8
fiber_lame = 8.0
fiber_shear = 5.0
relax_rate = 1.0 / 288.0
time_step = 0.25


def with_halo(cells, sides, width):
    for axis, dim in sides:
        count = lax.axis_size(axis)
        head = lax.slice_in_dim(cells, 0, width, axis=dim)
        tail = lax.slice_in_dim(cells, cells.shape[dim] - width, cells.shape[dim], axis=dim)
        cells = jnp.concatenate(
            [
                lax.ppermute(tail, axis, [(i, (i + 1) % count) for i in range(count)]),
                cells,
                lax.ppermute(head, axis, [((i + 1) % count, i) for i in range(count)]),
            ],
            axis=dim,
        )
    return cells


def from_behind(value, axis, steps):
    count = lax.axis_size(axis)
    pairs = [(source, (source + steps) % count) for source in range(count)]
    return lax.ppermute(value, axis, pairs)


def material_stress(grads, lame_field, shear_field, macro):
    eps11 = macro[0] + grads[0][0]
    eps22 = macro[1] + grads[1][1]
    eps33 = grads[2][2]
    eps12 = macro[2] + 0.5 * (grads[0][1] + grads[1][0])
    eps13 = 0.5 * (grads[0][2] + grads[2][0])
    eps23 = 0.5 * (grads[1][2] + grads[2][1])
    volume = lame_field * (eps11 + eps22 + eps33)
    twice = 2.0 * shear_field
    return (
        volume + twice * eps11,
        volume + twice * eps22,
        volume + twice * eps33,
        twice * eps12,
        twice * eps13,
        twice * eps23,
    )


def rotate_in(strain, cosine, sine):
    first, second, shear = (strain[0], strain[1], strain[2])
    return jnp.stack(
        [
            cosine * cosine * first + sine * sine * second + 2.0 * cosine * sine * shear,
            sine * sine * first + cosine * cosine * second - 2.0 * cosine * sine * shear,
            -cosine * sine * first
            + cosine * sine * second
            + (cosine * cosine - sine * sine) * shear,
        ]
    )


def rotate_out(stress, cosine, sine):
    first, second, shear = (stress[0], stress[1], stress[2])
    return jnp.stack(
        [
            cosine * cosine * first + sine * sine * second - 2.0 * cosine * sine * shear,
            sine * sine * first + cosine * cosine * second + 2.0 * cosine * sine * shear,
            cosine * sine * first
            - cosine * sine * second
            + (cosine * cosine - sine * sine) * shear,
        ]
    )


def back_diff(field, axis):
    if axis == 0:
        return field[1:] - field[:-1]
    return (field - jnp.roll(field, 1, axis))[1:]


def relax_slab(displace, lame_field, shear_field, macro):
    front = displace[:, :-1]
    grads = [
        [
            displace[i, 1:] - front[i],
            jnp.roll(front[i], -1, 1) - front[i],
            jnp.roll(front[i], -1, 2) - front[i],
        ]
        for i in range(3)
    ]
    s11, s22, s33, s12, s13, s23 = material_stress(grads, lame_field, shear_field, macro)
    first = back_diff(s11, 0) + back_diff(s12, 1) + back_diff(s13, 2)
    second = back_diff(s12, 0) + back_diff(s22, 1) + back_diff(s23, 2)
    third = back_diff(s13, 0) + back_diff(s23, 1) + back_diff(s33, 2)
    shifted = displace[:, 1:-1] + relax_rate * jnp.stack([first, second, third])
    return (shifted, (s11, s22, s12))


def share_planes(phase_planes, class_hot):
    fiber_share = phase_planes[0].astype(jnp.float32)[..., None] * class_hot[0]
    for class_number in range(1, NCLASS):
        fiber_share = (
            fiber_share
            + phase_planes[class_number].astype(jnp.float32)[..., None] * class_hot[class_number]
        )
    return fiber_share


def moduli_planes(phase_planes, class_hot):
    fiber_share = phase_planes[0].astype(jnp.float32)[..., None] * class_hot[0]
    for class_number in range(1, NCLASS):
        fiber_share = (
            fiber_share
            + phase_planes[class_number].astype(jnp.float32)[..., None] * class_hot[class_number]
        )
    lame_field = matrix_lame + (fiber_lame - matrix_lame) * fiber_share
    shear_field = matrix_shear + (fiber_shear - matrix_shear) * fiber_share
    return (lame_field, shear_field)


def slot_choice(target, tile_count, capacity, slots):
    highest = lax.Precision.HIGHEST
    row_count = target.shape[0]
    tile_hot = (target[:, None] == jnp.arange(tile_count, dtype=jnp.int32)[None, :]).astype(
        jnp.float32
    )
    row_ids = jnp.arange(row_count, dtype=jnp.int32)
    earlier_mask = (row_ids[:, None] > row_ids[None, :]).astype(jnp.float32)
    earlier = jnp.dot(earlier_mask, tile_hot, precision=highest)
    row_rank = jnp.sum(earlier * tile_hot, axis=1).astype(jnp.int32)
    slot_index = target * capacity + row_rank
    return (slot_index[:, None] == jnp.arange(slots, dtype=jnp.int32)[None, :]).astype(
        jnp.float32
    )


def tile_terms(choose, returned, cosine, sine, heights, elements, per_group):
    highest = lax.Precision.HIGHEST
    point_stress = jnp.dot(choose, returned, precision=highest)
    point_stress = point_stress.T.reshape(3, elements, per_group)
    global_stress = rotate_out(point_stress, cosine, sine)
    weight = 1.0 / TP
    forces = jnp.sum(global_stress, axis=2) * weight
    moments = jnp.sum(global_stress * heights[None, None, :], axis=2) * weight
    return jnp.concatenate([forces, moments], 0)


def node_forces(bmat, terms, connect, node_count):
    highest = lax.Precision.HIGHEST
    corner_force = jnp.einsum("akme,me->ake", bmat, terms, precision=highest)
    node_hot = (
        connect[:, :, None] == jnp.arange(node_count + GHOST, dtype=jnp.int32)[None, None, :]
    ).astype(jnp.float32)
    return jnp.einsum("ake,aen->kn", corner_force, node_hot, precision=highest)


def shift_rows(field, shift, axis):
    if axis == 1:
        size = field.shape[1]
        cut = (size - shift) % size
        return jnp.concatenate([field[:, cut:], field[:, :cut]], 1)
    return pltpu.roll(field, shift % field.shape[axis], axis)


def kernel_sweep(cells, lame_field, shear_field, macro):
    front = [part[:-1] for part in cells]
    grads = [
        [
            cells[i][1:] - front[i],
            shift_rows(front[i], -1, 1) - front[i],
            shift_rows(front[i], -1, 2) - front[i],
        ]
        for i in range(3)
    ]
    s11, s22, s33, s12, s13, s23 = material_stress(grads, lame_field, shear_field, macro)

    def diff(field, axis):
        if axis == 0:
            return field[1:] - field[:-1]
        return (field - shift_rows(field, 1, axis))[1:]

    first = diff(s11, 0) + diff(s12, 1) + diff(s13, 2)
    second = diff(s12, 0) + diff(s22, 1) + diff(s23, 2)
    third = diff(s13, 0) + diff(s23, 1) + diff(s33, 2)
    moved = [
        cells[i][1:-1] + relax_rate * rate_term
        for i, rate_term in enumerate((first, second, third))
    ]
    return (moved, (s11, s22, s12))


def relax_kernel(low_ref, state_ref, high_ref, share_ref, macro_ref, out_ref, mean_ref):
    rows = state_ref.shape[2]
    depth = ITERS

    def halo_planes(ref, component):
        return [
            ref[pl.ds((component * depth + p) * rows, rows)][None] for p in range(depth)
        ]

    cells = [
        jnp.concatenate(
            halo_planes(low_ref, i) + [state_ref[i]] + halo_planes(high_ref, i), 0
        )
        for i in range(3)
    ]
    fiber_share = share_ref[...]
    lame_all = matrix_lame + (fiber_lame - matrix_lame) * fiber_share
    shear_all = matrix_shear + (fiber_shear - matrix_shear) * fiber_share
    macro = [macro_ref[k : k + 1, :].reshape(1, 1, 1, -1) for k in range(3)]
    stress = None
    for round_number in range(ITERS):
        count = cells[0].shape[0]
        cells, stress = kernel_sweep(
            cells,
            lame_all[round_number : round_number + count - 1],
            shear_all[round_number : round_number + count - 1],
            macro,
        )
    for i in range(3):
        out_ref[i] = cells[i]
    lanes = mean_ref.shape[1]
    lane_from = lax.broadcasted_iota(jnp.int32, (lanes, lanes), 0)
    lane_to = lax.broadcasted_iota(jnp.int32, (lanes, lanes), 1)
    lane_shift = (lane_to == (lane_from + 2) % lanes).astype(jnp.float32)
    for k in range(3):
        total = jnp.sum(stress[k][1:], axis=(0, 1))
        mean_row = jnp.sum(total, axis=0, keepdims=True) / float(RES**3)
        mean_ref[k : k + 1, :] = mean_row
        mean_ref[3 + k : 4 + k, :] = jnp.dot(
            mean_row, lane_shift, precision=lax.Precision.HIGHEST, preferred_element_type=jnp.float32
        )


def relax_slab_kernel(low, state, high, fiber_share, macro):
    out_shape = (
        jax.ShapeDtypeStruct(state.shape, jnp.float32),
        jax.ShapeDtypeStruct((6, state.shape[-1]), jnp.float32),
    )
    return pl.pallas_call(
        relax_kernel,
        out_shape=out_shape,
        in_specs=[pl.BlockSpec(memory_space=pltpu.VMEM)] * 5,
        out_specs=(pl.BlockSpec(memory_space=pltpu.VMEM), pl.BlockSpec(memory_space=pltpu.VMEM)),
        compiler_params=pltpu.CompilerParams(vmem_limit_bytes=60 * 1024 * 1024),
    )(low, state, high, fiber_share, macro)


def halo_pack(cells, phase_planes):
    lanes = cells.shape[-1]
    rows = cells.shape[-2]
    flat_cells = cells.reshape(-1, rows, lanes)
    flat_phase = phase_planes.astype(jnp.float32).reshape(-1, rows, lanes)
    return jnp.concatenate([flat_cells, flat_phase], 0)


def halo_unpack(moved, phase_planes):
    count = moved.shape[0] - phase_planes.size // (moved.shape[1] * moved.shape[2])
    return moved[count:].reshape(phase_planes.shape).astype(jnp.int32)


def shards(
    gen_strain, ply_class, route, phase, rve_state, connect, bmat, velocity, force_ext, mass
):
    highest = lax.Precision.HIGHEST
    thick_index = lax.axis_index("thick")
    per_group = route.shape[2]
    elements = gen_strain.shape[1]
    tile_count = lax.axis_size("tile")
    slab_count = lax.axis_size("rve")
    slots = rve_state.shape[4]
    capacity = slots // tile_count
    row_count = elements * per_group
    depth = ITERS
    up = [(i, (i + 1) % slab_count) for i in range(slab_count)]
    down = [((i + 1) % slab_count, i) for i in range(slab_count)]
    planes = rve_state.shape[1]
    low_side = phase[:, planes - depth :]
    high_side = phase[:, :depth]
    pack_up = halo_pack(rve_state[:, planes - depth :], low_side)
    pack_down = halo_pack(rve_state[:, :depth], high_side)
    route_rows = route.reshape(elements, per_group).T
    int_rows = jnp.concatenate([route_rows, connect], 0)
    flat_bmat = bmat.reshape(-1, elements)
    layer = thick_index * per_group + jnp.arange(per_group, dtype=jnp.int32)
    heights = -1.0 + (2.0 * layer.astype(jnp.float32) + 1.0) / TP
    classes = lax.dynamic_slice_in_dim(ply_class, thick_index * per_group, per_group)
    angle = classes.astype(jnp.float32) * (math.pi / NCLASS)
    cosine = jnp.cos(angle)[None, :]
    sine = jnp.sin(angle)[None, :]
    membrane = gen_strain[:3][:, :, None]
    bending = gen_strain[3:][:, :, None]
    point_strain = membrane + heights[None, None, :] * bending
    rotated = rotate_in(point_strain, cosine, sine)
    row_class = jnp.broadcast_to(classes[None, :], (elements, per_group)).reshape(row_count)
    payload = jnp.concatenate(
        [rotated.reshape(3, row_count), row_class.astype(jnp.float32)[None, :]], 0
    ).T
    choose = slot_choice(route.reshape(row_count), tile_count, capacity, slots)
    send = jnp.dot(choose.T, payload, precision=highest)
    send, pack_up, pack_down = lax.optimization_barrier((send, pack_up, pack_down))
    below = lax.ppermute(pack_up, "rve", up)
    above = lax.ppermute(pack_down, "rve", down)
    phase_below = halo_unpack(below, low_side)
    phase_above = halo_unpack(above, high_side)
    received = lax.all_to_all(
        send.reshape(tile_count, capacity, 4), "tile", split_axis=0, concat_axis=0, tiled=True
    ).reshape(slots, 4)
    macro = received[:, :3].T
    slot_class = received[:, 3].astype(jnp.int32)
    class_hot = (slot_class[None, :] == jnp.arange(NCLASS, dtype=jnp.int32)[:, None]).astype(
        jnp.float32
    )
    wide_phase = jnp.concatenate([phase_below, phase, phase_above], 1)
    fiber_share = share_planes(wide_phase, class_hot)
    displace, average = relax_slab_kernel(below, rve_state, above, fiber_share, macro)
    ghost_rows = jnp.concatenate([flat_bmat, int_rows.astype(jnp.float32)], 0)
    ghost_rows, average = lax.optimization_barrier((ghost_rows, average))
    prev_pack = from_behind(ghost_rows, "tile", 1)
    both_chunks = (
        average.reshape(2, 3, tile_count, capacity)
        .transpose(2, 0, 3, 1)
        .reshape(tile_count, 2 * capacity, 3)
    )
    returned = lax.all_to_all(both_chunks, "tile", split_axis=0, concat_axis=0, tiled=True)
    own_returned = returned[:, :capacity].reshape(slots, 3)
    prev_returned = returned[:, capacity:].reshape(slots, 3)
    own_terms = tile_terms(choose, own_returned, cosine, sine, heights, elements, per_group)
    prev_bmat = prev_pack[: flat_bmat.shape[0]].reshape(bmat.shape)
    prev_ints = prev_pack[flat_bmat.shape[0] :].astype(jnp.int32)
    prev_route = prev_ints[:per_group].T.reshape(row_count)
    prev_connect = prev_ints[per_group:]
    prev_choose = slot_choice(prev_route, tile_count, capacity, slots)
    prev_terms = tile_terms(prev_choose, prev_returned, cosine, sine, heights, elements, per_group)
    node_count = velocity.shape[1]
    own_nodes = node_forces(bmat, own_terms, connect, node_count)[:, :node_count]
    ghost_nodes = node_forces(prev_bmat, prev_terms, prev_connect, node_count)[:, node_count:]
    partial_internal = own_nodes.at[:, :GHOST].add(ghost_nodes)
    totals = lax.psum(lax.psum(jnp.concatenate([own_terms, partial_internal], 0), "rve"), "thick")
    resultants = totals[:6]
    internal = totals[6:]
    new_velocity = velocity + time_step * (force_ext - internal) / mass[None, :]
    return (new_velocity, resultants, displace)


def solution(mesh):
    placed = (
        P(None, "tile"),
        P(),
        P("thick", "tile", None, None),
        P(None, "rve", None, None),
        P(None, "rve", None, None, ("tile", "thick")),
        P(None, "tile"),
        P(None, None, None, "tile"),
        P(None, "tile"),
        P(None, "tile"),
        P("tile"),
    )
    return jax.shard_map(
        shards,
        mesh=mesh,
        in_specs=placed,
        out_specs=(P(None, "tile"), P(None, "tile"), P(None, "rve", None, None, ("tile", "thick"))),
        check_vma=False,
    )
```

```python
import math

import jax
import jax.numpy as jnp
from jax import lax
from jax.experimental import pallas as pl
from jax.experimental.pallas import tpu as pltpu
from jax.sharding import PartitionSpec as P

TP = 8
NCLASS = 4
RES = 16
ITERS = 2
GHOST = 8


matrix_lame = 1.2
matrix_shear = 0.8
fiber_lame = 8.0
fiber_shear = 5.0
relax_rate = 1.0 / 288.0
time_step = 0.25


def with_halo(cells, sides, width):
    for axis, dim in sides:
        count = lax.axis_size(axis)
        head = lax.slice_in_dim(cells, 0, width, axis=dim)
        tail = lax.slice_in_dim(cells, cells.shape[dim] - width, cells.shape[dim], axis=dim)
        cells = jnp.concatenate(
            [
                lax.ppermute(tail, axis, [(i, (i + 1) % count) for i in range(count)]),
                cells,
                lax.ppermute(head, axis, [((i + 1) % count, i) for i in range(count)]),
            ],
            axis=dim,
        )
    return cells


def from_behind(value, axis, steps):
    count = lax.axis_size(axis)
    pairs = [(source, (source + steps) % count) for source in range(count)]
    return lax.ppermute(value, axis, pairs)


def material_stress(grads, lame_field, shear_field, macro):
    eps11 = macro[0] + grads[0][0]
    eps22 = macro[1] + grads[1][1]
    eps33 = grads[2][2]
    eps12 = macro[2] + 0.5 * (grads[0][1] + grads[1][0])
    eps13 = 0.5 * (grads[0][2] + grads[2][0])
    eps23 = 0.5 * (grads[1][2] + grads[2][1])
    volume = lame_field * (eps11 + eps22 + eps33)
    twice = 2.0 * shear_field
    return (
        volume + twice * eps11,
        volume + twice * eps22,
        volume + twice * eps33,
        twice * eps12,
        twice * eps13,
        twice * eps23,
    )


def rotate_in(strain, cosine, sine):
    first, second, shear = (strain[0], strain[1], strain[2])
    return jnp.stack(
        [
            cosine * cosine * first + sine * sine * second + 2.0 * cosine * sine * shear,
            sine * sine * first + cosine * cosine * second - 2.0 * cosine * sine * shear,
            -cosine * sine * first
            + cosine * sine * second
            + (cosine * cosine - sine * sine) * shear,
        ]
    )


def rotate_out(stress, cosine, sine):
    first, second, shear = (stress[0], stress[1], stress[2])
    return jnp.stack(
        [
            cosine * cosine * first + sine * sine * second - 2.0 * cosine * sine * shear,
            sine * sine * first + cosine * cosine * second + 2.0 * cosine * sine * shear,
            cosine * sine * first
            - cosine * sine * second
            + (cosine * cosine - sine * sine) * shear,
        ]
    )


def back_diff(field, axis):
    if axis == 0:
        return field[1:] - field[:-1]
    return (field - jnp.roll(field, 1, axis))[1:]


def relax_slab(displace, lame_field, shear_field, macro):
    front = displace[:, :-1]
    grads = [
        [
            displace[i, 1:] - front[i],
            jnp.roll(front[i], -1, 1) - front[i],
            jnp.roll(front[i], -1, 2) - front[i],
        ]
        for i in range(3)
    ]
    s11, s22, s33, s12, s13, s23 = material_stress(grads, lame_field, shear_field, macro)
    first = back_diff(s11, 0) + back_diff(s12, 1) + back_diff(s13, 2)
    second = back_diff(s12, 0) + back_diff(s22, 1) + back_diff(s23, 2)
    third = back_diff(s13, 0) + back_diff(s23, 1) + back_diff(s33, 2)
    shifted = displace[:, 1:-1] + relax_rate * jnp.stack([first, second, third])
    return (shifted, (s11, s22, s12))


def share_planes(phase_planes, class_hot):
    fiber_share = phase_planes[0].astype(jnp.float32)[..., None] * class_hot[0]
    for class_number in range(1, NCLASS):
        fiber_share = (
            fiber_share
            + phase_planes[class_number].astype(jnp.float32)[..., None] * class_hot[class_number]
        )
    return fiber_share


def moduli_planes(phase_planes, class_hot):
    fiber_share = phase_planes[0].astype(jnp.float32)[..., None] * class_hot[0]
    for class_number in range(1, NCLASS):
        fiber_share = (
            fiber_share
            + phase_planes[class_number].astype(jnp.float32)[..., None] * class_hot[class_number]
        )
    lame_field = matrix_lame + (fiber_lame - matrix_lame) * fiber_share
    shear_field = matrix_shear + (fiber_shear - matrix_shear) * fiber_share
    return (lame_field, shear_field)


def slot_choice(target, tile_count, capacity, slots):
    highest = lax.Precision.HIGHEST
    row_count = target.shape[0]
    tile_hot = (target[:, None] == jnp.arange(tile_count, dtype=jnp.int32)[None, :]).astype(
        jnp.float32
    )
    row_ids = jnp.arange(row_count, dtype=jnp.int32)
    earlier_mask = (row_ids[:, None] > row_ids[None, :]).astype(jnp.float32)
    earlier = jnp.dot(earlier_mask, tile_hot, precision=highest)
    row_rank = jnp.sum(earlier * tile_hot, axis=1).astype(jnp.int32)
    slot_index = target * capacity + row_rank
    return (slot_index[:, None] == jnp.arange(slots, dtype=jnp.int32)[None, :]).astype(
        jnp.float32
    )


def tile_terms(choose, returned, cosine, sine, heights, elements, per_group):
    highest = lax.Precision.HIGHEST
    point_stress = jnp.dot(choose, returned, precision=highest)
    point_stress = point_stress.T.reshape(3, elements, per_group)
    global_stress = rotate_out(point_stress, cosine, sine)
    weight = 1.0 / TP
    forces = jnp.sum(global_stress, axis=2) * weight
    moments = jnp.sum(global_stress * heights[None, None, :], axis=2) * weight
    return jnp.concatenate([forces, moments], 0)


def node_forces(bmat, terms, connect, node_count):
    highest = lax.Precision.HIGHEST
    corner_force = jnp.einsum("akme,me->ake", bmat, terms, precision=highest)
    node_hot = (
        connect[:, :, None] == jnp.arange(node_count + GHOST, dtype=jnp.int32)[None, None, :]
    ).astype(jnp.float32)
    return jnp.einsum("ake,aen->kn", corner_force, node_hot, precision=highest)


def shift_rows(field, shift, axis):
    if axis == 1:
        size = field.shape[1]
        cut = (size - shift) % size
        return jnp.concatenate([field[:, cut:], field[:, :cut]], 1)
    return pltpu.roll(field, shift % field.shape[axis], axis)


def kernel_sweep(cells, lame_field, shear_field, macro):
    front = [part[:-1] for part in cells]
    grads = [
        [
            cells[i][1:] - front[i],
            shift_rows(front[i], -1, 1) - front[i],
            shift_rows(front[i], -1, 2) - front[i],
        ]
        for i in range(3)
    ]
    s11, s22, s33, s12, s13, s23 = material_stress(grads, lame_field, shear_field, macro)

    def diff(field, axis):
        if axis == 0:
            return field[1:] - field[:-1]
        return (field - shift_rows(field, 1, axis))[1:]

    first = diff(s11, 0) + diff(s12, 1) + diff(s13, 2)
    second = diff(s12, 0) + diff(s22, 1) + diff(s23, 2)
    third = diff(s13, 0) + diff(s23, 1) + diff(s33, 2)
    moved = [
        cells[i][1:-1] + relax_rate * rate_term
        for i, rate_term in enumerate((first, second, third))
    ]
    return (moved, (s11, s22, s12))


def relax_kernel(low_ref, state_ref, high_ref, share_ref, macro_ref, out_ref, mean_ref):
    rows = state_ref.shape[2]
    depth = ITERS

    def halo_planes(ref, component):
        return [
            ref[pl.ds((component * depth + p) * rows, rows)][None] for p in range(depth)
        ]

    cells = [
        jnp.concatenate(
            halo_planes(low_ref, i) + [state_ref[i]] + halo_planes(high_ref, i), 0
        )
        for i in range(3)
    ]
    fiber_share = share_ref[...]
    lame_all = matrix_lame + (fiber_lame - matrix_lame) * fiber_share
    shear_all = matrix_shear + (fiber_shear - matrix_shear) * fiber_share
    macro = [macro_ref[k : k + 1, :].reshape(1, 1, 1, -1) for k in range(3)]
    stress = None
    for round_number in range(ITERS):
        count = cells[0].shape[0]
        cells, stress = kernel_sweep(
            cells,
            lame_all[round_number : round_number + count - 1],
            shear_all[round_number : round_number + count - 1],
            macro,
        )
    for i in range(3):
        out_ref[i] = cells[i]
    for k in range(3):
        total = jnp.sum(stress[k][1:], axis=(0, 1))
        mean_ref[k : k + 1, :] = jnp.sum(total, axis=0, keepdims=True) / float(RES**3)


def relax_slab_kernel(low, state, high, fiber_share, macro):
    out_shape = (
        jax.ShapeDtypeStruct(state.shape, jnp.float32),
        jax.ShapeDtypeStruct((3, state.shape[-1]), jnp.float32),
    )
    return pl.pallas_call(
        relax_kernel,
        out_shape=out_shape,
        in_specs=[pl.BlockSpec(memory_space=pltpu.VMEM)] * 5,
        out_specs=(pl.BlockSpec(memory_space=pltpu.VMEM), pl.BlockSpec(memory_space=pltpu.VMEM)),
        compiler_params=pltpu.CompilerParams(vmem_limit_bytes=60 * 1024 * 1024),
    )(low, state, high, fiber_share, macro)


def halo_pack(cells, phase_planes):
    lanes = cells.shape[-1]
    rows = cells.shape[-2]
    flat_cells = cells.reshape(-1, rows, lanes)
    flat_phase = phase_planes.astype(jnp.float32).reshape(-1, rows, lanes)
    return jnp.concatenate([flat_cells, flat_phase], 0)


def halo_unpack(moved, phase_planes):
    count = moved.shape[0] - phase_planes.size // (moved.shape[1] * moved.shape[2])
    return moved[count:].reshape(phase_planes.shape).astype(jnp.int32)


def shards(
    gen_strain, ply_class, route, phase, rve_state, connect, bmat, velocity, force_ext, mass
):
    highest = lax.Precision.HIGHEST
    thick_index = lax.axis_index("thick")
    per_group = route.shape[2]
    elements = gen_strain.shape[1]
    tile_count = lax.axis_size("tile")
    slab_count = lax.axis_size("rve")
    slots = rve_state.shape[4]
    capacity = slots // tile_count
    row_count = elements * per_group
    depth = ITERS
    up = [(i, (i + 1) % slab_count) for i in range(slab_count)]
    down = [((i + 1) % slab_count, i) for i in range(slab_count)]
    planes = rve_state.shape[1]
    low_side = phase[:, planes - depth :]
    high_side = phase[:, :depth]
    pack_up = halo_pack(rve_state[:, planes - depth :], low_side)
    pack_down = halo_pack(rve_state[:, :depth], high_side)
    route_rows = route.reshape(elements, per_group).T
    int_rows = jnp.concatenate([route_rows, connect], 0)
    flat_bmat = bmat.reshape(-1, elements)
    layer = thick_index * per_group + jnp.arange(per_group, dtype=jnp.int32)
    heights = -1.0 + (2.0 * layer.astype(jnp.float32) + 1.0) / TP
    classes = lax.dynamic_slice_in_dim(ply_class, thick_index * per_group, per_group)
    angle = classes.astype(jnp.float32) * (math.pi / NCLASS)
    cosine = jnp.cos(angle)[None, :]
    sine = jnp.sin(angle)[None, :]
    membrane = gen_strain[:3][:, :, None]
    bending = gen_strain[3:][:, :, None]
    point_strain = membrane + heights[None, None, :] * bending
    rotated = rotate_in(point_strain, cosine, sine)
    row_class = jnp.broadcast_to(classes[None, :], (elements, per_group)).reshape(row_count)
    payload = jnp.concatenate(
        [rotated.reshape(3, row_count), row_class.astype(jnp.float32)[None, :]], 0
    ).T
    choose = slot_choice(route.reshape(row_count), tile_count, capacity, slots)
    send = jnp.dot(choose.T, payload, precision=highest)
    send, pack_up, pack_down = lax.optimization_barrier((send, pack_up, pack_down))
    below = lax.ppermute(pack_up, "rve", up)
    above = lax.ppermute(pack_down, "rve", down)
    phase_below = halo_unpack(below, low_side)
    phase_above = halo_unpack(above, high_side)
    received = lax.all_to_all(
        send.reshape(tile_count, capacity, 4), "tile", split_axis=0, concat_axis=0, tiled=True
    ).reshape(slots, 4)
    macro = received[:, :3].T
    slot_class = received[:, 3].astype(jnp.int32)
    class_hot = (slot_class[None, :] == jnp.arange(NCLASS, dtype=jnp.int32)[:, None]).astype(
        jnp.float32
    )
    wide_phase = jnp.concatenate([phase_below, phase, phase_above], 1)
    fiber_share = share_planes(wide_phase, class_hot)
    displace, average = relax_slab_kernel(below, rve_state, above, fiber_share, macro)
    ghost_rows = jnp.concatenate([flat_bmat, int_rows.astype(jnp.float32)], 0)
    ghost_rows, average = lax.optimization_barrier((ghost_rows, average))
    prev_pack = from_behind(ghost_rows, "tile", 1)
    both_means = jnp.concatenate([average, jnp.roll(average, capacity, axis=1)], 0)
    both_chunks = (
        both_means.reshape(2, 3, tile_count, capacity)
        .transpose(2, 0, 3, 1)
        .reshape(tile_count, 2 * capacity, 3)
    )
    returned = lax.all_to_all(both_chunks, "tile", split_axis=0, concat_axis=0, tiled=True)
    own_returned = returned[:, :capacity].reshape(slots, 3)
    prev_returned = returned[:, capacity:].reshape(slots, 3)
    own_terms = tile_terms(choose, own_returned, cosine, sine, heights, elements, per_group)
    prev_bmat = prev_pack[: flat_bmat.shape[0]].reshape(bmat.shape)
    prev_ints = prev_pack[flat_bmat.shape[0] :].astype(jnp.int32)
    prev_route = prev_ints[:per_group].T.reshape(row_count)
    prev_connect = prev_ints[per_group:]
    prev_choose = slot_choice(prev_route, tile_count, capacity, slots)
    prev_terms = tile_terms(prev_choose, prev_returned, cosine, sine, heights, elements, per_group)
    node_count = velocity.shape[1]
    own_nodes = node_forces(bmat, own_terms, connect, node_count)[:, :node_count]
    ghost_nodes = node_forces(prev_bmat, prev_terms, prev_connect, node_count)[:, node_count:]
    partial_internal = own_nodes.at[:, :GHOST].add(ghost_nodes)
    totals = lax.psum(lax.psum(jnp.concatenate([own_terms, partial_internal], 0), "rve"), "thick")
    resultants = totals[:6]
    internal = totals[6:]
    new_velocity = velocity + time_step * (force_ext - internal) / mass[None, :]
    return (new_velocity, resultants, displace)


def solution(mesh):
    placed = (
        P(None, "tile"),
        P(),
        P("thick", "tile", None, None),
        P(None, "rve", None, None),
        P(None, "rve", None, None, ("tile", "thick")),
        P(None, "tile"),
        P(None, None, None, "tile"),
        P(None, "tile"),
        P(None, "tile"),
        P("tile"),
    )
    return jax.shard_map(
        shards,
        mesh=mesh,
        in_specs=placed,
        out_specs=(P(None, "tile"), P(None, "tile"), P(None, "rve", None, None, ("tile", "thick"))),
        check_vma=False,
    )
```
